32 devices in a mesh: groups: 2 (over y), seq: 16 (over z, x, core).
Axes of the slice: x: 2, y: 2, z: 4, core: 2. Of those that a mesh axis runs over, the one named last changes fastest.
Arguments:
- queries: bfloat16 [8192, 2048], P(('groups', 'seq')), parts along dimension 0, may hold values from -64 to 64
- keys: bfloat16 [8192, 2048], P(('groups', 'seq')), parts along dimension 0, may hold values from -6 to 6
- values: bfloat16 [8192, 2048], P(('groups', 'seq')), parts along dimension 0, may hold values from -6 to 6
- d_out: bfloat16 [8192, 2048], P(('groups', 'seq')), parts along dimension 0, may hold values from -6 to 6
- key_lists: int32 [64, 4], P(('groups', 'seq')), parts along dimension 0, may hold values from 0 to 31, as said below
Outputs:
- d_queries: bfloat16 [8192, 2048], P(('groups', 'seq')), parts along dimension 0
- d_keys: bfloat16 [8192, 2048], P(('groups', 'seq')), parts along dimension 0
- d_values: bfloat16 [8192, 2048], P(('groups', 'seq')), parts along dimension 0
The draws below stay inside these ranges and needn't reach their ends.
There are 2 independent parts, one for each index of `groups`. The reference program is written for one: setup_inputs(seed, part) draws one part's arguments, and reference() takes and returns one part's arrays. A program takes and returns all parts, laid end to end along the dimension named above; each array names one. Nothing has to cross between parts.
Inputs may be any that keep to these rules, and one draw needn't show every extreme that they name: `key_lists`: row b holds b, then (b - 1) modulo 32 if b is the first block of its aligned group of 2 blocks, (b + 1) modulo 32 if it is the last, else either of the two; then a block of the aligned group of 2 blocks that lies 4 groups before block b's group (cyclically), then a block of the group 4 groups after it (cyclically).
All inputs are finite; a program needn't handle non-finite values.
Results may differ from the reference program's by a relative error of at most 0.017.
Values may be sent and summed in bfloat16 or wider, within the bound.
No kernel may reach another device: no remote copies, remote signals or barrier semaphores. Data moves between devices by JAX's collectives and lax.ppermute only.
A program may use at most 128 MiB of HBM per device.

```python
import math
import jax
import jax.numpy as jnp
from jax import lax

BLK = 128
LOCAL_HEADS = 16
HEAD_SIZE = 128
NLIST = 4
FRAME_DEV = 4
BLK_DEV = 2
TOKENS = 4096


def query_key_pair(key):
    base = jax.random.fold_in(key, 7)
    first_key, second_key = jax.random.split(base)
    shape = (TOKENS, LOCAL_HEADS * HEAD_SIZE)
    key_raw = jax.random.truncated_normal(first_key, -6.0, 6.0, shape, jnp.float32)
    query_raw = jax.random.truncated_normal(second_key, -6.0, 6.0, shape, jnp.float32)
    return (query_raw, key_raw)


def draw_queries(key, part):
    return query_key_pair(key)[0].astype(jnp.bfloat16)


def draw_keys(key, part):
    return query_key_pair(key)[1].astype(jnp.bfloat16)


def draw_key_lists(key, part):
    nblocks = TOKENS // BLK
    ngroups = nblocks // BLK_DEV
    base = jax.random.fold_in(key, 3)
    side_key, early_key, late_key = jax.random.split(base, 3)
    block = jnp.arange(nblocks, dtype=jnp.int32)
    side = jax.random.randint(side_key, (nblocks,), 0, 2, dtype=jnp.int32)
    inner = block % BLK_DEV
    side = jnp.where(inner == 0, 0, jnp.where(inner == BLK_DEV - 1, 1, side))
    neighbour = (block + 2 * side - 1) % nblocks
    group = block // BLK_DEV
    earlier = (group - FRAME_DEV) % ngroups * BLK_DEV + jax.random.randint(early_key, (nblocks,), 0, BLK_DEV, dtype=jnp.int32)
    later = (group + FRAME_DEV) % ngroups * BLK_DEV + jax.random.randint(late_key, (nblocks,), 0, BLK_DEV, dtype=jnp.int32)
    return jnp.stack([block, neighbour, earlier, later], axis=1).astype(jnp.int32)


def shard_levels(own_key, extent, cuts, least, largest):
    factor_of, own = 1.0, jax.random.fold_in(own_key, 6)
    for axis_at, shards_of in cuts:
        steps = jnp.exp(jax.random.uniform(jax.random.fold_in(own, axis_at), (shards_of,), jnp.float32, least / len(cuts), largest / len(cuts)))
        factor_of = factor_of * jnp.repeat(steps, extent[axis_at] // shards_of).reshape([-1 if axis == axis_at else 1 for axis in range(len(extent))])
    return factor_of


def gaussian(stream_key, extent, spread, bound, cuts=(), held_as=jnp.bfloat16):
    values = spread * jax.random.normal(stream_key, extent, jnp.float32)
    if cuts:
        values = values * shard_levels(stream_key, extent, cuts, -0.22, 0.18)
    return jnp.clip(values, -bound, bound).astype(held_as)


def setup_inputs(seed: int = 0, part: int = 0) -> dict:
    seeds = jax.random.split(jax.random.key(seed), 6)
    own_keys = jax.random.split(jax.random.fold_in(seeds[5], part), 6)
    return {
        "queries": draw_queries(jax.random.fold_in(jax.random.fold_in(seeds[5], part), 71), part),
        "keys": draw_keys(jax.random.fold_in(jax.random.fold_in(seeds[5], part), 71), part),
        "values": gaussian(own_keys[2], (TOKENS, LOCAL_HEADS * HEAD_SIZE), 1.0, 6.0, ((0, 16),)),
        "d_out": gaussian(own_keys[3], (TOKENS, LOCAL_HEADS * HEAD_SIZE), 1.0, 6.0, ((0, 16),)),
        "key_lists": draw_key_lists(jax.random.fold_in(jax.random.fold_in(seeds[5], part), 71), part),
    }


def widen(array):
    return array.astype(jnp.float32)

def block_terms(query_block, grad_block, key_rows, value_rows):
    scale = 1.0 / math.sqrt(HEAD_SIZE)
    scores = jnp.einsum('qhd,khd->hqk', widen(query_block), widen(key_rows)) * scale
    top = lax.optimization_barrier(jnp.max(scores, axis=-1, keepdims=True))
    lse = top[..., 0] + jnp.log(lax.optimization_barrier(jnp.sum(jnp.exp(scores - top), axis=-1)))
    probs = jnp.exp(scores - lse[..., None])
    probs_low = lax.optimization_barrier(probs.astype(jnp.bfloat16))
    outputs = jnp.einsum('hqk,khd->hqd', widen(probs_low), widen(value_rows))
    delta = lax.optimization_barrier(jnp.sum(jnp.swapaxes(widen(grad_block), 0, 1) * outputs, axis=-1))
    d_probs = jnp.einsum('qhd,khd->hqk', widen(grad_block), widen(value_rows))
    d_scores = lax.optimization_barrier((probs * (d_probs - delta[..., None])).astype(jnp.bfloat16))
    d_query = (jnp.einsum('hqk,khd->qhd', widen(d_scores), widen(key_rows)) * scale).astype(jnp.bfloat16)
    d_value = jnp.einsum('hqk,qhd->khd', widen(probs_low), widen(grad_block))
    d_key = jnp.einsum('hqk,qhd->khd', widen(d_scores), widen(query_block)) * scale
    return (d_query, d_key, d_value)

def reference(queries, keys, values, d_out, key_lists):
    nblocks = key_lists.shape[0]
    width = queries.shape[1]
    query_all = queries.reshape(nblocks, BLK, LOCAL_HEADS, HEAD_SIZE)
    key_all = keys.reshape(nblocks, BLK, LOCAL_HEADS, HEAD_SIZE)
    value_all = values.reshape(nblocks, BLK, LOCAL_HEADS, HEAD_SIZE)
    grad_all = d_out.reshape(nblocks, BLK, LOCAL_HEADS, HEAD_SIZE)

    def step(carry, block):
        key_acc, value_acc = carry
        listed = key_lists[block]
        key_rows = key_all[listed].reshape(NLIST * BLK, LOCAL_HEADS, HEAD_SIZE)
        value_rows = value_all[listed].reshape(NLIST * BLK, LOCAL_HEADS, HEAD_SIZE)
        d_query, d_key, d_value = block_terms(query_all[block], grad_all[block], key_rows, value_rows)
        key_acc = key_acc.at[listed].add(d_key.reshape(NLIST, BLK, LOCAL_HEADS, HEAD_SIZE))
        value_acc = value_acc.at[listed].add(d_value.reshape(NLIST, BLK, LOCAL_HEADS, HEAD_SIZE))
        return ((key_acc, value_acc), d_query)
    zeros = jnp.zeros((nblocks, BLK, LOCAL_HEADS, HEAD_SIZE), jnp.float32)
    (key_acc, value_acc), d_queries = lax.scan(step, (zeros, zeros), jnp.arange(nblocks, dtype=jnp.int32))
    total = nblocks * BLK
    return (d_queries.reshape(total, width), key_acc.reshape(total, width).astype(jnp.bfloat16), value_acc.reshape(total, width).astype(jnp.bfloat16))
```

```python
import math

import jax
import jax.numpy as jnp
from jax import lax
from jax.experimental import pallas as pl
from jax.experimental.pallas import tpu as pltpu
from jax.sharding import PartitionSpec as P

BLK = 128
LOCAL_HEADS = 16
HEAD_SIZE = 128
FRAME_DEV = 4
BLK_DEV = 2

NT = (((1,), (1,)), ((), ()))
TN = (((0,), (0,)), ((), ()))
F32 = jnp.float32
BF16 = jnp.bfloat16


def shifted(tree, axis, distance):
    count = lax.axis_size(axis)
    route = [(i, (i + distance) % count) for i in range(count)]
    return lax.ppermute(tree, axis, route)


def row_block(ref, index):
    start = pl.multiple_of(index * BLK, BLK)
    return ref[pl.ds(start, BLK), :]


def query_kernel(kl_ref, q_ref, do_ref, k_ref, v_ref, lk_ref, lv_ref, rk_ref, rv_ref,
                 ek_ref, ev_ref, tk_ref, tv_ref, dq_ref, st_ref, *, scale):
    for i in range(BLK_DEV):
        rows = slice(i * BLK, (i + 1) * BLK)
        q = q_ref[rows, :]
        do = do_ref[rows, :]
        side_k, side_v = (lk_ref, lv_ref) if i == 0 else (rk_ref, rv_ref)
        early = lax.rem(kl_ref[i, 2], BLK_DEV)
        late = lax.rem(kl_ref[i, 3], BLK_DEV)
        keys = jnp.concatenate(
            [k_ref[rows, :], side_k[...], row_block(ek_ref, early), row_block(tk_ref, late)], axis=0
        )
        vals = jnp.concatenate(
            [v_ref[rows, :], side_v[...], row_block(ev_ref, early), row_block(tv_ref, late)], axis=0
        )
        s = lax.dot_general(keys, q, NT, preferred_element_type=F32) * scale
        top = jnp.max(s, axis=0, keepdims=True)
        lse = top + jnp.log(jnp.sum(jnp.exp(s - top), axis=0, keepdims=True))
        p = jnp.exp(s - lse)
        p_low = p.astype(BF16)
        dp = lax.dot_general(vals, do, NT, preferred_element_type=F32)
        delta = jnp.sum(p_low.astype(F32) * dp, axis=0, keepdims=True)
        ds = (p * (dp - delta)).astype(BF16)
        dq = lax.dot_general(ds, keys, TN, preferred_element_type=F32) * scale
        dq_ref[rows, :] = dq.astype(BF16)
        st_ref[0, 0:1, rows] = lse
        st_ref[0, 1:2, rows] = delta


def key_terms(keys, vals, q, do, lse, delta, scale):
    s = lax.dot_general(keys, q, NT, preferred_element_type=F32) * scale
    p = jnp.exp(s - lse)
    p_low = p.astype(BF16)
    dp = lax.dot_general(vals, do, NT, preferred_element_type=F32)
    ds = (p * (dp - delta)).astype(BF16)
    d_value = jnp.dot(p_low, do, preferred_element_type=F32)
    d_key = jnp.dot(ds, q, preferred_element_type=F32)
    return d_key, d_value


def key_kernel(klp_ref, klm_ref, k_ref, v_ref, q_ref, do_ref, st_ref,
               lq_ref, ldo_ref, lst_ref, rq_ref, rdo_ref, rst_ref,
               pq_ref, pdo_ref, pst_ref, mq_ref, mdo_ref, mst_ref,
               dk_ref, dv_ref, acc_k, acc_v, *, scale):
    sides = ((lq_ref, ldo_ref, lst_ref, 1), (rq_ref, rdo_ref, rst_ref, 0))
    for j in range(BLK_DEV):
        rows = slice(j * BLK, (j + 1) * BLK)
        side_q, side_do, side_st, side_blk = sides[j]
        far = slice(side_blk * BLK, (side_blk + 1) * BLK)
        q = jnp.concatenate([q_ref[rows, :], side_q[...]], axis=0)
        do = jnp.concatenate([do_ref[rows, :], side_do[...]], axis=0)
        lse = jnp.concatenate([st_ref[0, 0:1, rows], side_st[0, 0:1, far]], axis=1)
        delta = jnp.concatenate([st_ref[0, 1:2, rows], side_st[0, 1:2, far]], axis=1)
        d_key, d_value = key_terms(k_ref[rows, :], v_ref[rows, :], q, do, lse, delta, scale)
        acc_k[rows, :] = d_key
        acc_v[rows, :] = d_value
    for kl_ref, column, rq, rdo, rst in ((klp_ref, 2, pq_ref, pdo_ref, pst_ref),
                                         (klm_ref, 3, mq_ref, mdo_ref, mst_ref)):
        for r in range(BLK_DEV):
            rows = slice(r * BLK, (r + 1) * BLK)
            pick = lax.rem(kl_ref[r, column], BLK_DEV)
            start = pl.multiple_of(pick * BLK, BLK)
            mine = pl.ds(start, BLK)
            d_key, d_value = key_terms(
                k_ref[mine, :], v_ref[mine, :], rq[rows, :], rdo[rows, :],
                rst[0, 0:1, rows], rst[0, 1:2, rows], scale,
            )
            acc_k[mine, :] += d_key
            acc_v[mine, :] += d_value
    dk_ref[...] = (acc_k[...] * scale).astype(BF16)
    dv_ref[...] = acc_v[...].astype(BF16)


def body(queries, keys, values, d_out, key_lists):
    rows, width = queries.shape
    heads = width // HEAD_SIZE
    assert rows == BLK_DEV * BLK and key_lists.shape[0] == BLK_DEV
    scale = 1.0 / math.sqrt(HEAD_SIZE)

    tail = slice(rows - BLK, rows)
    head = slice(0, BLK)
    from_left = shifted(
        (keys[tail], values[tail], queries[tail], d_out[tail]), "seq", 1
    )
    from_right = shifted(
        (keys[head], values[head], queries[head], d_out[head]), "seq", -1
    )
    from_early = shifted((keys, values, queries, d_out, key_lists), "seq", FRAME_DEV)
    from_late = shifted((keys, values, queries, d_out, key_lists), "seq", -FRAME_DEV)

    full = pl.BlockSpec((rows, HEAD_SIZE), lambda h, *_: (0, h))
    edge = pl.BlockSpec((BLK, HEAD_SIZE), lambda h, *_: (0, h))
    stat = pl.BlockSpec((1, 2, rows), lambda h, *_: (h, 0, 0))

    d_queries, stats = pl.pallas_call(
        lambda *refs: query_kernel(*refs, scale=scale),
        grid_spec=pltpu.PrefetchScalarGridSpec(
            num_scalar_prefetch=1,
            grid=(heads,),
            in_specs=[full, full, full, full, edge, edge, edge, edge, full, full, full, full],
            out_specs=[full, stat],
        ),
        out_shape=[
            jax.ShapeDtypeStruct((rows, width), BF16),
            jax.ShapeDtypeStruct((heads, 2, rows), F32),
        ],
    )(
        key_lists, queries, d_out, keys, values,
        from_left[0], from_left[1], from_right[0], from_right[1],
        from_early[0], from_early[1], from_late[0], from_late[1],
    )

    stats_left = shifted(stats, "seq", 1)
    stats_right = shifted(stats, "seq", -1)
    stats_early = shifted(stats, "seq", FRAME_DEV)
    stats_late = shifted(stats, "seq", -FRAME_DEV)

    d_keys, d_values = pl.pallas_call(
        lambda *refs: key_kernel(*refs, scale=scale),
        grid_spec=pltpu.PrefetchScalarGridSpec(
            num_scalar_prefetch=2,
            grid=(heads,),
            in_specs=[full, full, full, full, stat,
                      edge, edge, stat, edge, edge, stat,
                      full, full, stat, full, full, stat],
            out_specs=[full, full],
            scratch_shapes=[pltpu.VMEM((rows, HEAD_SIZE), F32), pltpu.VMEM((rows, HEAD_SIZE), F32)],
        ),
        out_shape=[
            jax.ShapeDtypeStruct((rows, width), BF16),
            jax.ShapeDtypeStruct((rows, width), BF16),
        ],
    )(
        from_late[4], from_early[4],
        keys, values, queries, d_out, stats,
        from_left[2], from_left[3], stats_left,
        from_right[2], from_right[3], stats_right,
        from_late[2], from_late[3], stats_late,
        from_early[2], from_early[3], stats_early,
    )
    return (d_queries, d_keys, d_values)


def solution(mesh):
    spec = P(("groups", "seq"), None)
    return jax.shard_map(
        body,
        mesh=mesh,
        in_specs=(spec, spec, spec, spec, spec),
        out_specs=(spec, spec, spec),
        check_vma=False,
    )
```

```python
import math

import jax
import jax.numpy as jnp
from jax import lax
from jax.experimental import pallas as pl
from jax.experimental.pallas import tpu as pltpu
from jax.sharding import PartitionSpec as P

BLK = 128
LOCAL_HEADS = 16
HEAD_SIZE = 128
FRAME_DEV = 4
BLK_DEV = 2

NT = (((1,), (1,)), ((), ()))
TN = (((0,), (0,)), ((), ()))
F32 = jnp.float32
BF16 = jnp.bfloat16


def shifted(tree, axis, distance):
    count = lax.axis_size(axis)
    route = [(i, (i + distance) % count) for i in range(count)]
    return lax.ppermute(tree, axis, route)


def row_block(ref, index):
    start = pl.multiple_of(index * BLK, BLK)
    return ref[pl.ds(start, BLK), :]


def query_kernel(kl_ref, qd_ref, kv_ref, left_ref, right_ref, early_ref, late_ref,
                 dq_ref, st_ref, *, scale):
    for i in range(BLK_DEV):
        rows = slice(i * BLK, (i + 1) * BLK)
        q = qd_ref[0, rows, :]
        do = qd_ref[1, rows, :]
        side = left_ref if i == 0 else right_ref
        early = lax.rem(kl_ref[i, 2], BLK_DEV)
        late = lax.rem(kl_ref[i, 3], BLK_DEV)
        parts = []
        for n in range(2):
            parts.append(jnp.concatenate(
                [kv_ref[n, rows, :], side[n], row_block(early_ref.at[n], early),
                 row_block(late_ref.at[n], late)], axis=0
            ))
        keys, vals = parts
        s = lax.dot_general(keys, q, NT, preferred_element_type=F32) * scale
        top = jnp.max(s, axis=0, keepdims=True)
        lse = top + jnp.log(jnp.sum(jnp.exp(s - top), axis=0, keepdims=True))
        p = jnp.exp(s - lse)
        p_low = p.astype(BF16)
        dp = lax.dot_general(vals, do, NT, preferred_element_type=F32)
        delta = jnp.sum(p_low.astype(F32) * dp, axis=0, keepdims=True)
        ds = (p * (dp - delta)).astype(BF16)
        dq = lax.dot_general(ds, keys, TN, preferred_element_type=F32) * scale
        dq_ref[rows, :] = dq.astype(BF16)
        st_ref[0, 0:1, rows] = lse
        st_ref[0, 1:2, rows] = delta


def key_terms(keys, vals, q, do, lse, delta, scale):
    s = lax.dot_general(keys, q, NT, preferred_element_type=F32) * scale
    p = jnp.exp(s - lse)
    p_low = p.astype(BF16)
    dp = lax.dot_general(vals, do, NT, preferred_element_type=F32)
    ds = (p * (dp - delta)).astype(BF16)
    d_value = jnp.dot(p_low, do, preferred_element_type=F32)
    d_key = jnp.dot(ds, q, preferred_element_type=F32)
    return d_key, d_value


def near_kernel(kv_ref, qd_ref, st_ref, left_ref, lst_ref, right_ref, rst_ref, acc_ref, *, scale):
    sides = ((left_ref, lst_ref, 1), (right_ref, rst_ref, 0))
    for j in range(BLK_DEV):
        rows = slice(j * BLK, (j + 1) * BLK)
        side, side_st, side_blk = sides[j]
        far = slice(side_blk * BLK, (side_blk + 1) * BLK)
        q = jnp.concatenate([qd_ref[0, rows, :], side[0]], axis=0)
        do = jnp.concatenate([qd_ref[1, rows, :], side[1]], axis=0)
        lse = jnp.concatenate([st_ref[0, 0:1, rows], side_st[0, 0:1, far]], axis=1)
        delta = jnp.concatenate([st_ref[0, 1:2, rows], side_st[0, 1:2, far]], axis=1)
        d_key, d_value = key_terms(kv_ref[0, rows, :], kv_ref[1, rows, :], q, do, lse, delta, scale)
        acc_ref[0, rows, :] = d_key
        acc_ref[1, rows, :] = d_value


def far_kernel(klp_ref, klm_ref, kv_ref, acc_in, pqd_ref, pst_ref, mqd_ref, mst_ref,
               dk_ref, dv_ref, acc_k, acc_v, *, scale):
    acc_k[...] = acc_in[0]
    acc_v[...] = acc_in[1]
    for kl_ref, column, rqd, rst in ((klp_ref, 2, pqd_ref, pst_ref), (klm_ref, 3, mqd_ref, mst_ref)):
        for r in range(BLK_DEV):
            rows = slice(r * BLK, (r + 1) * BLK)
            pick = lax.rem(kl_ref[r, column], BLK_DEV)
            start = pl.multiple_of(pick * BLK, BLK)
            mine = pl.ds(start, BLK)
            d_key, d_value = key_terms(
                kv_ref[0, mine, :], kv_ref[1, mine, :], rqd[0, rows, :], rqd[1, rows, :],
                rst[0, 0:1, rows], rst[0, 1:2, rows], scale,
            )
            acc_k[mine, :] += d_key
            acc_v[mine, :] += d_value
    dk_ref[...] = (acc_k[...] * scale).astype(BF16)
    dv_ref[...] = acc_v[...].astype(BF16)


def body(queries, keys, values, d_out, key_lists):
    rows, width = queries.shape
    heads = width // HEAD_SIZE
    assert rows == BLK_DEV * BLK and key_lists.shape[0] == BLK_DEV
    scale = 1.0 / math.sqrt(HEAD_SIZE)

    kv = jnp.stack([keys, values])
    qd = jnp.stack([queries, d_out])
    tail = slice(rows - BLK, rows)
    head = slice(0, BLK)
    left_kv, left_qd = shifted((kv[:, tail], qd[:, tail]), "seq", 1)
    right_kv, right_qd = shifted((kv[:, head], qd[:, head]), "seq", -1)
    early_kv, early_kl = shifted((kv, key_lists), "seq", FRAME_DEV)
    late_kv, late_kl = shifted((kv, key_lists), "seq", -FRAME_DEV)
    first_phase = (qd, left_kv, left_qd, right_kv, right_qd, early_kv, early_kl, late_kv, late_kl)
    (qd_send, left_kv, left_qd, right_kv, right_qd, early_kv, early_kl, late_kv,
     late_kl) = lax.optimization_barrier(first_phase)
    early_qd = shifted(qd_send, "seq", FRAME_DEV)
    late_qd = shifted(qd_send, "seq", -FRAME_DEV)

    full = pl.BlockSpec((2, rows, HEAD_SIZE), lambda h, *_: (0, 0, h))
    edge = pl.BlockSpec((2, BLK, HEAD_SIZE), lambda h, *_: (0, 0, h))
    stat = pl.BlockSpec((1, 2, rows), lambda h, *_: (h, 0, 0))
    out = pl.BlockSpec((rows, HEAD_SIZE), lambda h, *_: (0, h))

    d_queries, stats = pl.pallas_call(
        lambda *refs: query_kernel(*refs, scale=scale),
        grid_spec=pltpu.PrefetchScalarGridSpec(
            num_scalar_prefetch=1,
            grid=(heads,),
            in_specs=[full, full, edge, edge, full, full],
            out_specs=[out, stat],
        ),
        out_shape=[
            jax.ShapeDtypeStruct((rows, width), BF16),
            jax.ShapeDtypeStruct((heads, 2, rows), F32),
        ],
    )(key_lists, qd, kv, left_kv, right_kv, early_kv, late_kv)

    stats_left = shifted(stats, "seq", 1)
    stats_right = shifted(stats, "seq", -1)
    stats_early = shifted(stats, "seq", FRAME_DEV)
    stats_late = shifted(stats, "seq", -FRAME_DEV)

    near = pl.pallas_call(
        lambda *refs: near_kernel(*refs, scale=scale),
        grid=(heads,),
        in_specs=[full, full, stat, edge, stat, edge, stat],
        out_specs=full,
        out_shape=jax.ShapeDtypeStruct((2, rows, width), F32),
    )(kv, qd, stats, left_qd, stats_left, right_qd, stats_right)

    d_keys, d_values = pl.pallas_call(
        lambda *refs: far_kernel(*refs, scale=scale),
        grid_spec=pltpu.PrefetchScalarGridSpec(
            num_scalar_prefetch=2,
            grid=(heads,),
            in_specs=[full, full, full, stat, full, stat],
            out_specs=[out, out],
            scratch_shapes=[pltpu.VMEM((rows, HEAD_SIZE), F32), pltpu.VMEM((rows, HEAD_SIZE), F32)],
        ),
        out_shape=[
            jax.ShapeDtypeStruct((rows, width), BF16),
            jax.ShapeDtypeStruct((rows, width), BF16),
        ],
    )(late_kl, early_kl, kv, near, late_qd, stats_late, early_qd, stats_early)
    return (d_queries, d_keys, d_values)


def solution(mesh):
    spec = P(("groups", "seq"), None)
    return jax.shard_map(
        body,
        mesh=mesh,
        in_specs=(spec, spec, spec, spec, spec),
        out_specs=(spec, spec, spec),
        check_vma=False,
    )
```

```python
import math

import jax
import jax.numpy as jnp
from jax import lax
from jax.experimental import pallas as pl
from jax.experimental.pallas import tpu as pltpu
from jax.sharding import PartitionSpec as P

BLK = 128
LOCAL_HEADS = 16
HEAD_SIZE = 128
FRAME_DEV = 4
BLK_DEV = 2

NT = (((1,), (1,)), ((), ()))
TN = (((0,), (0,)), ((), ()))
F32 = jnp.float32
BF16 = jnp.bfloat16


def shifted(tree, axis, distance):
    count = lax.axis_size(axis)
    route = [(i, (i + distance) % count) for i in range(count)]
    return lax.ppermute(tree, axis, route)


def row_block(ref, index):
    start = pl.multiple_of(index * BLK, BLK)
    return ref[pl.ds(start, BLK), :]


def query_kernel(kl_ref, qd_ref, kv_ref, left_ref, right_ref, early_ref, late_ref,
                 dq_ref, st_ref, *, scale):
    for i in range(BLK_DEV):
        rows = slice(i * BLK, (i + 1) * BLK)
        q = qd_ref[0, rows, :]
        do = qd_ref[1, rows, :]
        side = left_ref if i == 0 else right_ref
        early = lax.rem(kl_ref[i, 2], BLK_DEV)
        late = lax.rem(kl_ref[i, 3], BLK_DEV)
        parts = []
        for n in range(2):
            parts.append(jnp.concatenate(
                [kv_ref[n, rows, :], side[n], row_block(early_ref.at[n], early),
                 row_block(late_ref.at[n], late)], axis=0
            ))
        keys, vals = parts
        s = lax.dot_general(keys, q, NT, preferred_element_type=F32) * scale
        top = jnp.max(s, axis=0, keepdims=True)
        lse = top + jnp.log(jnp.sum(jnp.exp(s - top), axis=0, keepdims=True))
        p = jnp.exp(s - lse)
        p_low = p.astype(BF16)
        dp = lax.dot_general(vals, do, NT, preferred_element_type=F32)
        delta = jnp.sum(p_low.astype(F32) * dp, axis=0, keepdims=True)
        ds = (p * (dp - delta)).astype(BF16)
        dq = lax.dot_general(ds, keys, TN, preferred_element_type=F32) * scale
        dq_ref[rows, :] = dq.astype(BF16)
        st_ref[0, 0:1, rows] = lse
        st_ref[0, 1:2, rows] = delta
        st_ref[0, 2:3, rows] = jnp.full((1, BLK), early.astype(F32), F32)
        st_ref[0, 3:4, rows] = jnp.full((1, BLK), late.astype(F32), F32)


def key_terms(keys, vals, q, do, lse, delta, scale):
    s = lax.dot_general(keys, q, NT, preferred_element_type=F32) * scale
    p = jnp.exp(s - lse)
    p_low = p.astype(BF16)
    dp = lax.dot_general(vals, do, NT, preferred_element_type=F32)
    ds = (p * (dp - delta)).astype(BF16)
    d_value = jnp.dot(p_low, do, preferred_element_type=F32)
    d_key = jnp.dot(ds, q, preferred_element_type=F32)
    return d_key, d_value


def near_kernel(kv_ref, qd_ref, st_ref, left_ref, lst_ref, right_ref, rst_ref, acc_ref, *, scale):
    sides = ((left_ref, lst_ref, 1), (right_ref, rst_ref, 0))
    for j in range(BLK_DEV):
        rows = slice(j * BLK, (j + 1) * BLK)
        side, side_st, side_blk = sides[j]
        far = slice(side_blk * BLK, (side_blk + 1) * BLK)
        q = jnp.concatenate([qd_ref[0, rows, :], side[0]], axis=0)
        do = jnp.concatenate([qd_ref[1, rows, :], side[1]], axis=0)
        lse = jnp.concatenate([st_ref[0, 0:1, rows], side_st[0, 0:1, far]], axis=1)
        delta = jnp.concatenate([st_ref[0, 1:2, rows], side_st[0, 1:2, far]], axis=1)
        d_key, d_value = key_terms(kv_ref[0, rows, :], kv_ref[1, rows, :], q, do, lse, delta, scale)
        acc_ref[0, rows, :] = d_key
        acc_ref[1, rows, :] = d_value


def far_kernel(kv_ref, acc_in, rqd_ref, rst_ref, *outs, scale, column, last):
    acc = [[acc_in[n, j * BLK:(j + 1) * BLK, :] for j in range(BLK_DEV)] for n in range(2)]
    for r in range(BLK_DEV):
        rows = slice(r * BLK, (r + 1) * BLK)
        pick = rst_ref[0, column:column + 1, rows]
        first = pick == 0.0
        keys = jnp.where(first, kv_ref[0, 0:BLK, :], kv_ref[0, BLK:2 * BLK, :])
        vals = jnp.where(first, kv_ref[1, 0:BLK, :], kv_ref[1, BLK:2 * BLK, :])
        terms = key_terms(
            keys, vals, rqd_ref[0, rows, :], rqd_ref[1, rows, :],
            rst_ref[0, 0:1, rows], rst_ref[0, 1:2, rows], scale,
        )
        for n in range(2):
            acc[n][0] = acc[n][0] + jnp.where(first, terms[n], 0.0)
            acc[n][1] = acc[n][1] + jnp.where(first, 0.0, terms[n])
    if last:
        dk_ref, dv_ref = outs
        for j in range(BLK_DEV):
            rows = slice(j * BLK, (j + 1) * BLK)
            dk_ref[rows, :] = (acc[0][j] * scale).astype(BF16)
            dv_ref[rows, :] = acc[1][j].astype(BF16)
    else:
        (acc_out,) = outs
        for n in range(2):
            for j in range(BLK_DEV):
                acc_out[n, j * BLK:(j + 1) * BLK, :] = acc[n][j]


def cost(heads, block_products, exp_blocks, bytes_accessed):
    flops = 2 * BLK * BLK * HEAD_SIZE * block_products * heads
    return pl.CostEstimate(
        flops=flops, transcendentals=BLK * BLK * exp_blocks * heads, bytes_accessed=bytes_accessed
    )


def body(queries, keys, values, d_out, key_lists):
    rows, width = queries.shape
    heads = width // HEAD_SIZE
    assert rows == BLK_DEV * BLK and key_lists.shape[0] == BLK_DEV
    scale = 1.0 / math.sqrt(HEAD_SIZE)

    kv = jnp.stack([keys, values])
    qd = jnp.stack([queries, d_out])
    tail = slice(rows - BLK, rows)
    head = slice(0, BLK)
    left_kv, left_qd = shifted((kv[:, tail], qd[:, tail]), "seq", 1)
    right_kv, right_qd = shifted((kv[:, head], qd[:, head]), "seq", -1)
    kv_send, qd_send, left_kv, left_qd, right_kv, right_qd = lax.optimization_barrier(
        (kv, qd, left_kv, left_qd, right_kv, right_qd)
    )
    early_kv = shifted(kv_send, "seq", FRAME_DEV)
    late_kv = shifted(kv_send, "seq", -FRAME_DEV)
    late_qd = shifted(qd_send, "seq", -FRAME_DEV)

    full = pl.BlockSpec((2, rows, HEAD_SIZE), lambda h, *_: (0, 0, h))
    edge = pl.BlockSpec((2, BLK, HEAD_SIZE), lambda h, *_: (0, 0, h))
    stat = pl.BlockSpec((1, 4, rows), lambda h, *_: (h, 0, 0))
    out = pl.BlockSpec((rows, HEAD_SIZE), lambda h, *_: (0, h))

    d_queries, stats = pl.pallas_call(
        lambda *refs: query_kernel(*refs, scale=scale),
        grid_spec=pltpu.PrefetchScalarGridSpec(
            num_scalar_prefetch=1,
            grid=(heads,),
            in_specs=[full, full, edge, edge, full, full],
            out_specs=[out, stat],
        ),
        out_shape=[
            jax.ShapeDtypeStruct((rows, width), BF16),
            jax.ShapeDtypeStruct((heads, 4, rows), F32),
        ],
        cost_estimate=cost(heads, 24, 8, 14 * rows * width),
    )(key_lists, qd, kv, left_kv, right_kv, early_kv, late_kv)

    stats_left = shifted(stats, "seq", 1)
    stats_right = shifted(stats, "seq", -1)
    stats_early = shifted(stats, "seq", FRAME_DEV)
    stats_late = shifted(stats, "seq", -FRAME_DEV)
    qd_send, stats_left, stats_right, stats_early, stats_late = lax.optimization_barrier(
        (qd, stats_left, stats_right, stats_early, stats_late)
    )
    early_qd = shifted(qd_send, "seq", FRAME_DEV)

    near = pl.pallas_call(
        lambda *refs: near_kernel(*refs, scale=scale),
        grid=(heads,),
        in_specs=[full, full, stat, edge, stat, edge, stat],
        out_specs=full,
        out_shape=jax.ShapeDtypeStruct((2, rows, width), F32),
        cost_estimate=cost(heads, 16, 4, 14 * rows * width),
    )(kv, qd, stats, left_qd, stats_left, right_qd, stats_right)

    near = pl.pallas_call(
        lambda *refs: far_kernel(*refs, scale=scale, column=2, last=False),
        grid=(heads,),
        in_specs=[full, full, full, stat],
        out_specs=full,
        out_shape=jax.ShapeDtypeStruct((2, rows, width), F32),
        input_output_aliases={1: 0},
        cost_estimate=cost(heads, 8, 2, 16 * rows * width),
    )(kv, near, late_qd, stats_late)

    d_keys, d_values = pl.pallas_call(
        lambda *refs: far_kernel(*refs, scale=scale, column=3, last=True),
        grid=(heads,),
        in_specs=[full, full, full, stat],
        out_specs=[out, out],
        out_shape=[
            jax.ShapeDtypeStruct((rows, width), BF16),
            jax.ShapeDtypeStruct((rows, width), BF16),
        ],
        cost_estimate=cost(heads, 8, 2, 16 * rows * width),
    )(kv, near, early_qd, stats_early)
    return (d_queries, d_keys, d_values)


def solution(mesh):
    spec = P(("groups", "seq"), None)
    return jax.shard_map(
        body,
        mesh=mesh,
        in_specs=(spec, spec, spec, spec, spec),
        out_specs=(spec, spec, spec),
        check_vma=False,
    )
```

```python
import math

import jax
import jax.numpy as jnp
from jax import lax
from jax.experimental import pallas as pl
from jax.experimental.pallas import tpu as pltpu
from jax.sharding import PartitionSpec as P

BLK = 128
LOCAL_HEADS = 16
HEAD_SIZE = 128
FRAME_DEV = 4
BLK_DEV = 2
STEP_HEADS = 4

NT = (((1,), (1,)), ((), ()))
TN = (((0,), (0,)), ((), ()))
F32 = jnp.float32
BF16 = jnp.bfloat16


def shifted(tree, axis, distance):
    count = lax.axis_size(axis)
    route = [(i, (i + distance) % count) for i in range(count)]
    return lax.ppermute(tree, axis, route)


def cols(hh):
    return slice(hh * HEAD_SIZE, (hh + 1) * HEAD_SIZE)


def row_block(ref, index, hh):
    start = pl.multiple_of(index * BLK, BLK)
    return ref[pl.ds(start, BLK), cols(hh)]


def query_kernel(kl_ref, qd_ref, kv_ref, left_ref, right_ref, early_ref, late_ref,
                 dq_ref, st_ref, *, scale):
    for i in range(BLK_DEV):
        rows = slice(i * BLK, (i + 1) * BLK)
        side = left_ref if i == 0 else right_ref
        early = lax.rem(kl_ref[i, 2], BLK_DEV)
        late = lax.rem(kl_ref[i, 3], BLK_DEV)
        for hh in range(STEP_HEADS):
            c = cols(hh)
            q = qd_ref[0, rows, c]
            do = qd_ref[1, rows, c]
            parts = []
            for n in range(2):
                parts.append(jnp.concatenate(
                    [kv_ref[n, rows, c], side[n, :, c], row_block(early_ref.at[n], early, hh),
                     row_block(late_ref.at[n], late, hh)], axis=0
                ))
            keys, vals = parts
            s = lax.dot_general(keys, q, NT, preferred_element_type=F32) * scale
            top = jnp.max(s, axis=0, keepdims=True)
            lse = top + jnp.log(jnp.sum(jnp.exp(s - top), axis=0, keepdims=True))
            p = jnp.exp(s - lse)
            p_low = p.astype(BF16)
            dp = lax.dot_general(vals, do, NT, preferred_element_type=F32)
            delta = jnp.sum(p_low.astype(F32) * dp, axis=0, keepdims=True)
            ds = (p * (dp - delta)).astype(BF16)
            dq = lax.dot_general(ds, keys, TN, preferred_element_type=F32) * scale
            dq_ref[rows, c] = dq.astype(BF16)
            st_ref[hh, 0:1, rows] = lse
            st_ref[hh, 1:2, rows] = delta
            st_ref[hh, 2:3, rows] = jnp.full((1, BLK), early.astype(F32), F32)
            st_ref[hh, 3:4, rows] = jnp.full((1, BLK), late.astype(F32), F32)


def key_terms(keys, vals, q, do, lse, delta, scale):
    s = lax.dot_general(keys, q, NT, preferred_element_type=F32) * scale
    p = jnp.exp(s - lse)
    p_low = p.astype(BF16)
    dp = lax.dot_general(vals, do, NT, preferred_element_type=F32)
    ds = (p * (dp - delta)).astype(BF16)
    d_value = jnp.dot(p_low, do, preferred_element_type=F32)
    d_key = jnp.dot(ds, q, preferred_element_type=F32)
    return d_key, d_value


def near_kernel(kv_ref, qd_ref, st_ref, left_ref, lst_ref, right_ref, rst_ref, acc_ref, *, scale):
    sides = ((left_ref, lst_ref, 1), (right_ref, rst_ref, 0))
    for j in range(BLK_DEV):
        rows = slice(j * BLK, (j + 1) * BLK)
        side, side_st, side_blk = sides[j]
        far = slice(side_blk * BLK, (side_blk + 1) * BLK)
        for hh in range(STEP_HEADS):
            c = cols(hh)
            q = jnp.concatenate([qd_ref[0, rows, c], side[0, :, c]], axis=0)
            do = jnp.concatenate([qd_ref[1, rows, c], side[1, :, c]], axis=0)
            lse = jnp.concatenate([st_ref[hh, 0:1, rows], side_st[hh, 0:1, far]], axis=1)
            delta = jnp.concatenate([st_ref[hh, 1:2, rows], side_st[hh, 1:2, far]], axis=1)
            d_key, d_value = key_terms(kv_ref[0, rows, c], kv_ref[1, rows, c], q, do, lse, delta, scale)
            acc_ref[0, rows, c] = d_key
            acc_ref[1, rows, c] = d_value


def far_kernel(kv_ref, acc_in, rqd_ref, rst_ref, *outs, scale, column, last):
    for hh in range(STEP_HEADS):
        c = cols(hh)
        acc = [[acc_in[n, j * BLK:(j + 1) * BLK, c] for j in range(BLK_DEV)] for n in range(2)]
        for r in range(BLK_DEV):
            rows = slice(r * BLK, (r + 1) * BLK)
            first = rst_ref[hh, column:column + 1, rows] == 0.0
            keys = jnp.where(first, kv_ref[0, 0:BLK, c], kv_ref[0, BLK:2 * BLK, c])
            vals = jnp.where(first, kv_ref[1, 0:BLK, c], kv_ref[1, BLK:2 * BLK, c])
            terms = key_terms(
                keys, vals, rqd_ref[0, rows, c], rqd_ref[1, rows, c],
                rst_ref[hh, 0:1, rows], rst_ref[hh, 1:2, rows], scale,
            )
            for n in range(2):
                acc[n][0] = acc[n][0] + jnp.where(first, terms[n], 0.0)
                acc[n][1] = acc[n][1] + jnp.where(first, 0.0, terms[n])
        for j in range(BLK_DEV):
            rows = slice(j * BLK, (j + 1) * BLK)
            if last:
                dk_ref, dv_ref = outs
                dk_ref[rows, c] = (acc[0][j] * scale).astype(BF16)
                dv_ref[rows, c] = acc[1][j].astype(BF16)
            else:
                (acc_out,) = outs
                acc_out[0, rows, c] = acc[0][j]
                acc_out[1, rows, c] = acc[1][j]


def cost(steps, block_products, exp_blocks, bytes_accessed):
    heads = steps * STEP_HEADS
    flops = 2 * BLK * BLK * HEAD_SIZE * block_products * heads
    return pl.CostEstimate(
        flops=flops, transcendentals=BLK * BLK * exp_blocks * heads, bytes_accessed=bytes_accessed
    )


def body(queries, keys, values, d_out, key_lists):
    rows, width = queries.shape
    steps = width // (HEAD_SIZE * STEP_HEADS)
    assert rows == BLK_DEV * BLK and key_lists.shape[0] == BLK_DEV
    assert steps * HEAD_SIZE * STEP_HEADS == width
    scale = 1.0 / math.sqrt(HEAD_SIZE)

    kvqd = jnp.stack([keys, values, queries, d_out])
    left = shifted(kvqd[:, rows - BLK:], "seq", 1)
    right = shifted(kvqd[:, :BLK], "seq", -1)
    kvqd_send, left, right = lax.optimization_barrier((kvqd, left, right))
    early_kv = shifted(kvqd_send[:2], "seq", FRAME_DEV)
    late = shifted(kvqd_send, "seq", -FRAME_DEV)
    qd_send, early_kv, late = lax.optimization_barrier((kvqd[2:], early_kv, late))

    width_step = HEAD_SIZE * STEP_HEADS
    first = pl.BlockSpec((2, rows, width_step), lambda h, *_: (0, 0, h))
    second = pl.BlockSpec((2, rows, width_step), lambda h, *_: (1, 0, h))
    edge_first = pl.BlockSpec((2, BLK, width_step), lambda h, *_: (0, 0, h))
    edge_second = pl.BlockSpec((2, BLK, width_step), lambda h, *_: (1, 0, h))
    stat = pl.BlockSpec((STEP_HEADS, 4, rows), lambda h, *_: (h, 0, 0))
    out = pl.BlockSpec((rows, width_step), lambda h, *_: (0, h))
    heads = steps * STEP_HEADS
    array_bytes = rows * width * 2

    d_queries, stats = pl.pallas_call(
        lambda *refs: query_kernel(*refs, scale=scale),
        grid_spec=pltpu.PrefetchScalarGridSpec(
            num_scalar_prefetch=1,
            grid=(steps,),
            in_specs=[second, first, edge_first, edge_first, first, first],
            out_specs=[out, stat],
        ),
        out_shape=[
            jax.ShapeDtypeStruct((rows, width), BF16),
            jax.ShapeDtypeStruct((heads, 4, rows), F32),
        ],
        cost_estimate=cost(steps, 24, 8, 11 * array_bytes),
    )(key_lists, kvqd, kvqd, left, right, early_kv, late)

    stats_left = shifted(stats, "seq", 1)
    stats_right = shifted(stats, "seq", -1)
    stats_early = shifted(stats, "seq", FRAME_DEV)
    stats_late = shifted(stats, "seq", -FRAME_DEV)
    qd_send, stats_left, stats_right, stats_early, stats_late = lax.optimization_barrier(
        (qd_send, stats_left, stats_right, stats_early, stats_late)
    )
    early_qd = shifted(qd_send, "seq", FRAME_DEV)

    near = pl.pallas_call(
        lambda *refs: near_kernel(*refs, scale=scale),
        grid=(steps,),
        in_specs=[first, second, stat, edge_second, stat, edge_second, stat],
        out_specs=first,
        out_shape=jax.ShapeDtypeStruct((2, rows, width), F32),
        cost_estimate=cost(steps, 16, 4, 10 * array_bytes),
    )(kvqd, kvqd, stats, left, stats_left, right, stats_right)

    near = pl.pallas_call(
        lambda *refs: far_kernel(*refs, scale=scale, column=2, last=False),
        grid=(steps,),
        in_specs=[first, first, second, stat],
        out_specs=first,
        out_shape=jax.ShapeDtypeStruct((2, rows, width), F32),
        input_output_aliases={1: 0},
        cost_estimate=cost(steps, 8, 2, 12 * array_bytes),
    )(kvqd, near, late, stats_late)

    d_keys, d_values = pl.pallas_call(
        lambda *refs: far_kernel(*refs, scale=scale, column=3, last=True),
        grid=(steps,),
        in_specs=[first, first, first, stat],
        out_specs=[out, out],
        out_shape=[
            jax.ShapeDtypeStruct((rows, width), BF16),
            jax.ShapeDtypeStruct((rows, width), BF16),
        ],
        cost_estimate=cost(steps, 8, 2, 10 * array_bytes),
    )(kvqd, near, early_qd, stats_early)
    return (d_queries, d_keys, d_values)


def solution(mesh):
    spec = P(("groups", "seq"), None)
    return jax.shard_map(
        body,
        mesh=mesh,
        in_specs=(spec, spec, spec, spec, spec),
        out_specs=(spec, spec, spec),
        check_vma=False,
    )
```

```python
import math

import jax
import jax.numpy as jnp
from jax import lax
from jax.experimental import pallas as pl
from jax.experimental.pallas import tpu as pltpu
from jax.sharding import PartitionSpec as P

BLK = 128
LOCAL_HEADS = 16
HEAD_SIZE = 128
FRAME_DEV = 4
BLK_DEV = 2
STEP_HEADS = 4

NT = (((1,), (1,)), ((), ()))
TN = (((0,), (0,)), ((), ()))
F32 = jnp.float32
BF16 = jnp.bfloat16


def shifted(tree, axis, distance):
    count = lax.axis_size(axis)
    route = [(i, (i + distance) % count) for i in range(count)]
    return lax.ppermute(tree, axis, route)


def cols(hh):
    return slice(hh * HEAD_SIZE, (hh + 1) * HEAD_SIZE)


def picked(index):
    return pl.ds(pl.multiple_of(index * BLK, BLK), BLK)


def attend_kernel(kl_ref, qd_ref, kv_ref, left_ref, right_ref, early_ref, late_ref,
                  dq_ref, own_ref, to_left, to_right, to_early, to_late, acc_early, acc_late,
                  *, scale):
    acc_early[...] = jnp.zeros_like(acc_early)
    acc_late[...] = jnp.zeros_like(acc_late)
    for i in range(BLK_DEV):
        rows = slice(i * BLK, (i + 1) * BLK)
        side = left_ref if i == 0 else right_ref
        to_side = to_left if i == 0 else to_right
        early = lax.rem(kl_ref[i, 2], BLK_DEV)
        late = lax.rem(kl_ref[i, 3], BLK_DEV)
        for hh in range(STEP_HEADS):
            c = cols(hh)
            q = qd_ref[0, rows, c]
            do = qd_ref[1, rows, c]
            parts = []
            for n in range(2):
                parts.append(jnp.concatenate(
                    [kv_ref[n, rows, c], side[n, :, c], early_ref[n, picked(early), c],
                     late_ref[n, picked(late), c]], axis=0
                ))
            keys, vals = parts
            s = lax.dot_general(keys, q, NT, preferred_element_type=F32) * scale
            top = jnp.max(s, axis=0, keepdims=True)
            lse = top + jnp.log(jnp.sum(jnp.exp(s - top), axis=0, keepdims=True))
            p = jnp.exp(s - lse)
            p_low = p.astype(BF16)
            dp = lax.dot_general(vals, do, NT, preferred_element_type=F32)
            delta = jnp.sum(p_low.astype(F32) * dp, axis=0, keepdims=True)
            ds = (p * (dp - delta)).astype(BF16)
            dq = lax.dot_general(ds, keys, TN, preferred_element_type=F32) * scale
            dq_ref[rows, c] = dq.astype(BF16)
            d_key = jnp.dot(ds, q, preferred_element_type=F32) * scale
            d_value = jnp.dot(p_low, do, preferred_element_type=F32)
            for n, term in ((0, d_key), (1, d_value)):
                own_ref[n, rows, c] = term[0:BLK]
                to_side[n, :, c] = term[BLK:2 * BLK].astype(BF16)
                acc_early[n, picked(early), c] += term[2 * BLK:3 * BLK]
                acc_late[n, picked(late), c] += term[3 * BLK:4 * BLK]
    to_early[...] = acc_early[...].astype(BF16)
    to_late[...] = acc_late[...].astype(BF16)


def body(queries, keys, values, d_out, key_lists):
    rows, width = queries.shape
    steps = width // (HEAD_SIZE * STEP_HEADS)
    assert rows == BLK_DEV * BLK and key_lists.shape[0] == BLK_DEV
    assert steps * HEAD_SIZE * STEP_HEADS == width
    scale = 1.0 / math.sqrt(HEAD_SIZE)

    kv = jnp.stack([keys, values])
    qd = jnp.stack([queries, d_out])
    left = shifted(kv[:, rows - BLK:], "seq", 1)
    right = shifted(kv[:, :BLK], "seq", -1)
    kv_send, left, right = lax.optimization_barrier((kv, left, right))
    early = shifted(kv_send, "seq", FRAME_DEV)
    late = shifted(kv_send, "seq", -FRAME_DEV)

    width_step = HEAD_SIZE * STEP_HEADS
    pair = pl.BlockSpec((2, rows, width_step), lambda h, *_: (0, 0, h))
    edge = pl.BlockSpec((2, BLK, width_step), lambda h, *_: (0, 0, h))
    out = pl.BlockSpec((rows, width_step), lambda h, *_: (0, h))
    heads = steps * STEP_HEADS
    flops = 2 * BLK * 4 * BLK * HEAD_SIZE * 5 * BLK_DEV * heads
    cost = pl.CostEstimate(
        flops=flops, transcendentals=2 * BLK * 4 * BLK * BLK_DEV * heads,
        bytes_accessed=14 * rows * width * 2,
    )

    d_queries, own, to_left, to_right, to_early, to_late = pl.pallas_call(
        lambda *refs: attend_kernel(*refs, scale=scale),
        grid_spec=pltpu.PrefetchScalarGridSpec(
            num_scalar_prefetch=1,
            grid=(steps,),
            in_specs=[pair, pair, edge, edge, pair, pair],
            out_specs=[out, pair, edge, edge, pair, pair],
            scratch_shapes=[pltpu.VMEM((2, rows, width_step), F32)] * 2,
        ),
        out_shape=[
            jax.ShapeDtypeStruct((rows, width), BF16),
            jax.ShapeDtypeStruct((2, rows, width), F32),
            jax.ShapeDtypeStruct((2, BLK, width), BF16),
            jax.ShapeDtypeStruct((2, BLK, width), BF16),
            jax.ShapeDtypeStruct((2, rows, width), BF16),
            jax.ShapeDtypeStruct((2, rows, width), BF16),
        ],
        cost_estimate=cost,
    )(key_lists, qd, kv, left, right, early, late)

    from_right = shifted(to_left, "seq", -1)
    from_left = shifted(to_right, "seq", 1)
    from_late = shifted(to_early, "seq", -FRAME_DEV)
    from_early = shifted(to_late, "seq", FRAME_DEV)
    side = jnp.concatenate([from_left, from_right], axis=1).astype(F32)
    total = own + side + from_late.astype(F32) + from_early.astype(F32)
    grads = total.astype(BF16)
    return (d_queries, grads[0], grads[1])


def solution(mesh):
    spec = P(("groups", "seq"), None)
    return jax.shard_map(
        body,
        mesh=mesh,
        in_specs=(spec, spec, spec, spec, spec),
        out_specs=(spec, spec, spec),
        check_vma=False,
    )
```

```python
import math

import jax
import jax.numpy as jnp
from jax import lax
from jax.experimental import pallas as pl
from jax.experimental.pallas import tpu as pltpu
from jax.sharding import PartitionSpec as P

BLK = 128
LOCAL_HEADS = 16
HEAD_SIZE = 128
FRAME_DEV = 4
BLK_DEV = 2
STEP_HEADS = 4
CHUNK_STEPS = (3, 1)

NT = (((1,), (1,)), ((), ()))
TN = (((0,), (0,)), ((), ()))
F32 = jnp.float32
BF16 = jnp.bfloat16


def shifted(tree, axis, distance):
    count = lax.axis_size(axis)
    route = [(i, (i + distance) % count) for i in range(count)]
    return lax.ppermute(tree, axis, route)


def cols(hh):
    return slice(hh * HEAD_SIZE, (hh + 1) * HEAD_SIZE)


def picked(index):
    return pl.ds(pl.multiple_of(index * BLK, BLK), BLK)


def attend_kernel(kl_ref, qd_ref, kv_ref, left_ref, right_ref, early_ref, late_ref, *rest,
                  scale, aliased):
    if aliased:
        rest = rest[2:]
    dq_ref, own_ref, to_left, to_right, to_early, to_late, acc_early, acc_late = rest
    acc_early[...] = jnp.zeros_like(acc_early)
    acc_late[...] = jnp.zeros_like(acc_late)
    for i in range(BLK_DEV):
        rows = slice(i * BLK, (i + 1) * BLK)
        side = left_ref if i == 0 else right_ref
        to_side = to_left if i == 0 else to_right
        early = lax.rem(kl_ref[i, 2], BLK_DEV)
        late = lax.rem(kl_ref[i, 3], BLK_DEV)
        for hh in range(STEP_HEADS):
            c = cols(hh)
            q = qd_ref[0, rows, c]
            do = qd_ref[1, rows, c]
            parts = []
            for n in range(2):
                parts.append(jnp.concatenate(
                    [kv_ref[n, rows, c], side[n, :, c], early_ref[n, picked(early), c],
                     late_ref[n, picked(late), c]], axis=0
                ))
            keys, vals = parts
            s = lax.dot_general(keys, q, NT, preferred_element_type=F32) * scale
            top = jnp.max(s, axis=0, keepdims=True)
            lse = top + jnp.log(jnp.sum(jnp.exp(s - top), axis=0, keepdims=True))
            p = jnp.exp(s - lse)
            p_low = p.astype(BF16)
            dp = lax.dot_general(vals, do, NT, preferred_element_type=F32)
            delta = jnp.sum(p_low.astype(F32) * dp, axis=0, keepdims=True)
            ds = (p * (dp - delta)).astype(BF16)
            dq = lax.dot_general(ds, keys, TN, preferred_element_type=F32) * scale
            dq_ref[rows, c] = dq.astype(BF16)
            d_key = jnp.dot(ds, q, preferred_element_type=F32) * scale
            d_value = jnp.dot(p_low, do, preferred_element_type=F32)
            for n, term in ((0, d_key), (1, d_value)):
                own_ref[n, rows, c] = term[0:BLK]
                to_side[n, :, c] = term[BLK:2 * BLK].astype(BF16)
                acc_early[n, picked(early), c] += term[2 * BLK:3 * BLK]
                acc_late[n, picked(late), c] += term[3 * BLK:4 * BLK]
    to_early[...] = acc_early[...].astype(BF16)
    to_late[...] = acc_late[...].astype(BF16)


def body(queries, keys, values, d_out, key_lists):
    rows, width = queries.shape
    steps = width // (HEAD_SIZE * STEP_HEADS)
    assert rows == BLK_DEV * BLK and key_lists.shape[0] == BLK_DEV
    assert steps * HEAD_SIZE * STEP_HEADS == width
    scale = 1.0 / math.sqrt(HEAD_SIZE)

    kv = jnp.stack([keys, values])
    qd = jnp.stack([queries, d_out])
    width_step = HEAD_SIZE * STEP_HEADS
    assert sum(CHUNK_STEPS) == steps
    bases = [sum(CHUNK_STEPS[:c]) for c in range(len(CHUNK_STEPS))]
    chunked = [kv[:, :, b * width_step:(b + n) * width_step] for b, n in zip(bases, CHUNK_STEPS)]
    left = shifted(kv[:, rows - BLK:], "seq", 1)
    right = shifted(kv[:, :BLK], "seq", -1)
    chunked, left, right = lax.optimization_barrier((chunked, left, right))
    far = []
    for part in chunked:
        far.append((shifted(part, "seq", FRAME_DEV), shifted(part, "seq", -FRAME_DEV)))

    d_queries = own = None
    received = []
    for c, (base, chunk_steps) in enumerate(zip(bases, CHUNK_STEPS)):
        chunk_width = chunk_steps * width_step
        heads = chunk_steps * STEP_HEADS
        cost = pl.CostEstimate(
            flops=2 * BLK * 4 * BLK * HEAD_SIZE * 5 * BLK_DEV * heads,
            transcendentals=2 * BLK * 4 * BLK * BLK_DEV * heads,
            bytes_accessed=14 * rows * chunk_width * 2,
        )
        pair = pl.BlockSpec((2, rows, width_step), lambda h, *_, b=base: (0, 0, b + h))
        edge = pl.BlockSpec((2, BLK, width_step), lambda h, *_, b=base: (0, 0, b + h))
        out = pl.BlockSpec((rows, width_step), lambda h, *_, b=base: (0, b + h))
        local_pair = pl.BlockSpec((2, rows, width_step), lambda h, *_: (0, 0, h))
        local_edge = pl.BlockSpec((2, BLK, width_step), lambda h, *_: (0, 0, h))
        aliased = c > 0
        extra_specs = [pl.BlockSpec(memory_space=pl.ANY)] * 2 if aliased else []
        extra_args = [d_queries, own] if aliased else []
        aliases = {7: 0, 8: 1} if aliased else {}
        d_queries, own, to_left, to_right, to_early, to_late = pl.pallas_call(
            lambda *refs, a=aliased: attend_kernel(*refs, scale=scale, aliased=a),
            grid_spec=pltpu.PrefetchScalarGridSpec(
                num_scalar_prefetch=1,
                grid=(chunk_steps,),
                in_specs=[pair, pair, edge, edge, local_pair, local_pair] + extra_specs,
                out_specs=[out, pair, local_edge, local_edge, local_pair, local_pair],
                scratch_shapes=[pltpu.VMEM((2, rows, width_step), F32)] * 2,
            ),
            out_shape=[
                jax.ShapeDtypeStruct((rows, width), BF16),
                jax.ShapeDtypeStruct((2, rows, width), F32),
                jax.ShapeDtypeStruct((2, BLK, chunk_width), BF16),
                jax.ShapeDtypeStruct((2, BLK, chunk_width), BF16),
                jax.ShapeDtypeStruct((2, rows, chunk_width), BF16),
                jax.ShapeDtypeStruct((2, rows, chunk_width), BF16),
            ],
            input_output_aliases=aliases,
            cost_estimate=cost,
        )(key_lists, qd, kv, left, right, far[c][0], far[c][1], *extra_args)
        received.append((
            shifted(to_right, "seq", 1), shifted(to_left, "seq", -1),
            shifted(to_late, "seq", FRAME_DEV), shifted(to_early, "seq", -FRAME_DEV),
        ))
    from_left, from_right, from_early, from_late = (
        jnp.concatenate([r[k] for r in received], axis=-1) for k in range(4)
    )
    side = jnp.concatenate([from_left, from_right], axis=1).astype(F32)
    total = own + side + from_late.astype(F32) + from_early.astype(F32)
    grads = total.astype(BF16)
    return (d_queries, grads[0], grads[1])


def solution(mesh):
    spec = P(("groups", "seq"), None)
    return jax.shard_map(
        body,
        mesh=mesh,
        in_specs=(spec, spec, spec, spec, spec),
        out_specs=(spec, spec, spec),
        check_vma=False,
    )
```

```python
import math

import jax
import jax.numpy as jnp
from jax import lax
from jax.experimental import pallas as pl
from jax.experimental.pallas import tpu as pltpu
from jax.sharding import PartitionSpec as P

BLK = 128
LOCAL_HEADS = 16
HEAD_SIZE = 128
FRAME_DEV = 4
BLK_DEV = 2
STEP_HEADS = 4
CHUNK_STEPS = (3, 1)

NT = (((1,), (1,)), ((), ()))
TN = (((0,), (0,)), ((), ()))
F32 = jnp.float32
BF16 = jnp.bfloat16


def shifted(tree, axis, distance):
    count = lax.axis_size(axis)
    route = [(i, (i + distance) % count) for i in range(count)]
    return lax.ppermute(tree, axis, route)


def cols(hh):
    return slice(hh * HEAD_SIZE, (hh + 1) * HEAD_SIZE)


def picked(index):
    return pl.ds(pl.multiple_of(index * BLK, BLK), BLK)


def attend_kernel(kl_ref, qd_ref, kv_ref, left_ref, right_ref, early_ref, late_ref, *rest,
                  scale, aliased):
    if aliased:
        rest = rest[2:]
    dq_ref, own_ref, to_left, to_right, to_early, to_late, acc_early, acc_late = rest
    acc_early[...] = jnp.zeros_like(acc_early)
    acc_late[...] = jnp.zeros_like(acc_late)
    for i in range(BLK_DEV):
        rows = slice(i * BLK, (i + 1) * BLK)
        side = left_ref if i == 0 else right_ref
        to_side = to_left if i == 0 else to_right
        early = lax.rem(kl_ref[i, 2], BLK_DEV)
        late = lax.rem(kl_ref[i, 3], BLK_DEV)
        for hh in range(STEP_HEADS):
            c = cols(hh)
            q = qd_ref[0, rows, c]
            do = qd_ref[1, rows, c]
            parts = []
            for n in range(2):
                parts.append(jnp.concatenate(
                    [kv_ref[n, rows, c], side[n, :, c], early_ref[n, picked(early), c],
                     late_ref[n, picked(late), c]], axis=0
                ))
            keys, vals = parts
            s = lax.dot_general(keys, q, NT, preferred_element_type=F32) * scale
            top = jnp.max(s, axis=0, keepdims=True)
            lse = top + jnp.log(jnp.sum(jnp.exp(s - top), axis=0, keepdims=True))
            p = jnp.exp(s - lse)
            p_low = p.astype(BF16)
            dp = lax.dot_general(vals, do, NT, preferred_element_type=F32)
            delta = jnp.sum(p_low.astype(F32) * dp, axis=0, keepdims=True)
            ds = (p * (dp - delta)).astype(BF16)
            dq = lax.dot_general(ds, keys, TN, preferred_element_type=F32) * scale
            dq_ref[rows, c] = dq.astype(BF16)
            d_key = jnp.dot(ds, q, preferred_element_type=F32) * scale
            d_value = jnp.dot(p_low, do, preferred_element_type=F32)
            for n, term in ((0, d_key), (1, d_value)):
                own_ref[n, rows, c] = term[0:BLK]
                to_side[n, :, c] = term[BLK:2 * BLK].astype(BF16)
                acc_early[n, picked(early), c] += term[2 * BLK:3 * BLK]
                acc_late[n, picked(late), c] += term[3 * BLK:4 * BLK]
    to_early[...] = acc_early[...].astype(BF16)
    to_late[...] = acc_late[...].astype(BF16)


def body(queries, keys, values, d_out, key_lists):
    rows, width = queries.shape
    steps = width // (HEAD_SIZE * STEP_HEADS)
    assert rows == BLK_DEV * BLK and key_lists.shape[0] == BLK_DEV
    assert steps * HEAD_SIZE * STEP_HEADS == width
    scale = 1.0 / math.sqrt(HEAD_SIZE)

    kv = jnp.stack([keys, values])
    qd = jnp.stack([queries, d_out])
    width_step = HEAD_SIZE * STEP_HEADS
    assert sum(CHUNK_STEPS) == steps
    bases = [sum(CHUNK_STEPS[:c]) for c in range(len(CHUNK_STEPS))]
    chunked = [kv[:, :, b * width_step:(b + n) * width_step] for b, n in zip(bases, CHUNK_STEPS)]
    far = []
    for part in chunked:
        far.append((shifted(part, "seq", FRAME_DEV), shifted(part, "seq", -FRAME_DEV)))
    left = shifted(kv[:, rows - BLK:], "seq", 1)
    right = shifted(kv[:, :BLK], "seq", -1)

    d_queries = own = None
    received = []
    for c, (base, chunk_steps) in enumerate(zip(bases, CHUNK_STEPS)):
        chunk_width = chunk_steps * width_step
        heads = chunk_steps * STEP_HEADS
        cost = pl.CostEstimate(
            flops=2 * BLK * 4 * BLK * HEAD_SIZE * 5 * BLK_DEV * heads,
            transcendentals=2 * BLK * 4 * BLK * BLK_DEV * heads,
            bytes_accessed=14 * rows * chunk_width * 2,
        )
        pair = pl.BlockSpec((2, rows, width_step), lambda h, *_, b=base: (0, 0, b + h))
        edge = pl.BlockSpec((2, BLK, width_step), lambda h, *_, b=base: (0, 0, b + h))
        out = pl.BlockSpec((rows, width_step), lambda h, *_, b=base: (0, b + h))
        local_pair = pl.BlockSpec((2, rows, width_step), lambda h, *_: (0, 0, h))
        local_edge = pl.BlockSpec((2, BLK, width_step), lambda h, *_: (0, 0, h))
        aliased = c > 0
        extra_specs = [pl.BlockSpec(memory_space=pl.ANY)] * 2 if aliased else []
        extra_args = [d_queries, own] if aliased else []
        aliases = {7: 0, 8: 1} if aliased else {}
        d_queries, own, to_left, to_right, to_early, to_late = pl.pallas_call(
            lambda *refs, a=aliased: attend_kernel(*refs, scale=scale, aliased=a),
            grid_spec=pltpu.PrefetchScalarGridSpec(
                num_scalar_prefetch=1,
                grid=(chunk_steps,),
                in_specs=[pair, pair, edge, edge, local_pair, local_pair] + extra_specs,
                out_specs=[out, pair, local_edge, local_edge, local_pair, local_pair],
                scratch_shapes=[pltpu.VMEM((2, rows, width_step), F32)] * 2,
            ),
            out_shape=[
                jax.ShapeDtypeStruct((rows, width), BF16),
                jax.ShapeDtypeStruct((2, rows, width), F32),
                jax.ShapeDtypeStruct((2, BLK, chunk_width), BF16),
                jax.ShapeDtypeStruct((2, BLK, chunk_width), BF16),
                jax.ShapeDtypeStruct((2, rows, chunk_width), BF16),
                jax.ShapeDtypeStruct((2, rows, chunk_width), BF16),
            ],
            input_output_aliases=aliases,
            cost_estimate=cost,
        )(key_lists, qd, kv, left, right, far[c][0], far[c][1], *extra_args)
        received.append((
            shifted(to_right, "seq", 1), shifted(to_left, "seq", -1),
            shifted(to_late, "seq", FRAME_DEV), shifted(to_early, "seq", -FRAME_DEV),
        ))
    from_left, from_right, from_early, from_late = (
        jnp.concatenate([r[k] for r in received], axis=-1) for k in range(4)
    )
    side = jnp.concatenate([from_left, from_right], axis=1).astype(F32)
    total = own + side + from_late.astype(F32) + from_early.astype(F32)
    grads = total.astype(BF16)
    return (d_queries, grads[0], grads[1])


def solution(mesh):
    spec = P(("groups", "seq"), None)
    return jax.shard_map(
        body,
        mesh=mesh,
        in_specs=(spec, spec, spec, spec, spec),
        out_specs=(spec, spec, spec),
        check_vma=False,
    )
```

```python
import math

import jax
import jax.numpy as jnp
from jax import lax
from jax.experimental import pallas as pl
from jax.experimental.pallas import tpu as pltpu
from jax.sharding import Mesh, PartitionSpec as P

BLK = 128
LOCAL_HEADS = 16
HEAD_SIZE = 128
FRAME_DEV = 4
BLK_DEV = 2
STEP_HEADS = 4
CHUNK_STEPS = (3, 1)

NT = (((1,), (1,)), ((), ()))
TN = (((0,), (0,)), ((), ()))
F32 = jnp.float32
BF16 = jnp.bfloat16


SEQ = ("pair", "core")


def crossing(tree):
    count = lax.axis_size(SEQ)
    route = [(i, (i - 1 if i % 2 == 0 else i + 1) % count) for i in range(count)]
    return lax.ppermute(tree, SEQ, route)


def swap_edges(for_left, for_right):
    core = lax.axis_index("core")
    even = core == 0
    across = crossing(jnp.where(even, for_left, for_right))
    gathered = lax.all_gather(jnp.where(even, for_right, for_left), "core")
    partner = lax.dynamic_index_in_dim(gathered, 1 - core, keepdims=False)
    return jnp.where(even, across, partner), jnp.where(even, partner, across)


def shifted(tree, axis, distance):
    count = lax.axis_size(axis)
    route = [(i, (i + distance) % count) for i in range(count)]
    return lax.ppermute(tree, axis, route)


def cols(hh):
    return slice(hh * HEAD_SIZE, (hh + 1) * HEAD_SIZE)


def picked(index):
    return pl.ds(pl.multiple_of(index * BLK, BLK), BLK)


def attend_kernel(kl_ref, qd_ref, kv_ref, left_ref, right_ref, early_ref, late_ref, *rest,
                  scale, aliased):
    if aliased:
        rest = rest[2:]
    dq_ref, own_ref, to_left, to_right, to_early, to_late, acc_early, acc_late = rest
    acc_early[...] = jnp.zeros_like(acc_early)
    acc_late[...] = jnp.zeros_like(acc_late)
    for i in range(BLK_DEV):
        rows = slice(i * BLK, (i + 1) * BLK)
        side = left_ref if i == 0 else right_ref
        to_side = to_left if i == 0 else to_right
        early = lax.rem(kl_ref[i, 2], BLK_DEV)
        late = lax.rem(kl_ref[i, 3], BLK_DEV)
        for hh in range(STEP_HEADS):
            c = cols(hh)
            q = qd_ref[0, rows, c]
            do = qd_ref[1, rows, c]
            parts = []
            for n in range(2):
                parts.append(jnp.concatenate(
                    [kv_ref[n, rows, c], side[n, :, c], early_ref[n, picked(early), c],
                     late_ref[n, picked(late), c]], axis=0
                ))
            keys, vals = parts
            s = lax.dot_general(keys, q, NT, preferred_element_type=F32) * scale
            top = jnp.max(s, axis=0, keepdims=True)
            lse = top + jnp.log(jnp.sum(jnp.exp(s - top), axis=0, keepdims=True))
            p = jnp.exp(s - lse)
            p_low = p.astype(BF16)
            dp = lax.dot_general(vals, do, NT, preferred_element_type=F32)
            delta = jnp.sum(p_low.astype(F32) * dp, axis=0, keepdims=True)
            ds = (p * (dp - delta)).astype(BF16)
            dq = lax.dot_general(ds, keys, TN, preferred_element_type=F32) * scale
            dq_ref[rows, c] = dq.astype(BF16)
            d_key = jnp.dot(ds, q, preferred_element_type=F32) * scale
            d_value = jnp.dot(p_low, do, preferred_element_type=F32)
            for n, term in ((0, d_key), (1, d_value)):
                own_ref[n, rows, c] = term[0:BLK]
                to_side[n, :, c] = term[BLK:2 * BLK].astype(BF16)
                acc_early[n, picked(early), c] += term[2 * BLK:3 * BLK]
                acc_late[n, picked(late), c] += term[3 * BLK:4 * BLK]
    to_early[...] = acc_early[...].astype(BF16)
    to_late[...] = acc_late[...].astype(BF16)


def body(queries, keys, values, d_out, key_lists):
    rows, width = queries.shape
    steps = width // (HEAD_SIZE * STEP_HEADS)
    assert rows == BLK_DEV * BLK and key_lists.shape[0] == BLK_DEV
    assert steps * HEAD_SIZE * STEP_HEADS == width
    scale = 1.0 / math.sqrt(HEAD_SIZE)

    kv = jnp.stack([keys, values])
    qd = jnp.stack([queries, d_out])
    width_step = HEAD_SIZE * STEP_HEADS
    assert sum(CHUNK_STEPS) == steps
    bases = [sum(CHUNK_STEPS[:c]) for c in range(len(CHUNK_STEPS))]
    chunked = [kv[:, :, b * width_step:(b + n) * width_step] for b, n in zip(bases, CHUNK_STEPS)]
    far = []
    for part in chunked:
        far.append((shifted(part, SEQ, FRAME_DEV), shifted(part, SEQ, -FRAME_DEV)))
    left, right = swap_edges(kv[:, :BLK], kv[:, rows - BLK:])

    d_queries = own = None
    received = []
    for c, (base, chunk_steps) in enumerate(zip(bases, CHUNK_STEPS)):
        chunk_width = chunk_steps * width_step
        heads = chunk_steps * STEP_HEADS
        cost = pl.CostEstimate(
            flops=2 * BLK * 4 * BLK * HEAD_SIZE * 5 * BLK_DEV * heads,
            transcendentals=2 * BLK * 4 * BLK * BLK_DEV * heads,
            bytes_accessed=14 * rows * chunk_width * 2,
        )
        pair = pl.BlockSpec((2, rows, width_step), lambda h, *_, b=base: (0, 0, b + h))
        edge = pl.BlockSpec((2, BLK, width_step), lambda h, *_, b=base: (0, 0, b + h))
        out = pl.BlockSpec((rows, width_step), lambda h, *_, b=base: (0, b + h))
        local_pair = pl.BlockSpec((2, rows, width_step), lambda h, *_: (0, 0, h))
        local_edge = pl.BlockSpec((2, BLK, width_step), lambda h, *_: (0, 0, h))
        aliased = c > 0
        extra_specs = [pl.BlockSpec(memory_space=pl.ANY)] * 2 if aliased else []
        extra_args = [d_queries, own] if aliased else []
        aliases = {7: 0, 8: 1} if aliased else {}
        d_queries, own, to_left, to_right, to_early, to_late = pl.pallas_call(
            lambda *refs, a=aliased: attend_kernel(*refs, scale=scale, aliased=a),
            grid_spec=pltpu.PrefetchScalarGridSpec(
                num_scalar_prefetch=1,
                grid=(chunk_steps,),
                in_specs=[pair, pair, edge, edge, local_pair, local_pair] + extra_specs,
                out_specs=[out, pair, local_edge, local_edge, local_pair, local_pair],
                scratch_shapes=[pltpu.VMEM((2, rows, width_step), F32)] * 2,
            ),
            out_shape=[
                jax.ShapeDtypeStruct((rows, width), BF16),
                jax.ShapeDtypeStruct((2, rows, width), F32),
                jax.ShapeDtypeStruct((2, BLK, chunk_width), BF16),
                jax.ShapeDtypeStruct((2, BLK, chunk_width), BF16),
                jax.ShapeDtypeStruct((2, rows, chunk_width), BF16),
                jax.ShapeDtypeStruct((2, rows, chunk_width), BF16),
            ],
            input_output_aliases=aliases,
            cost_estimate=cost,
        )(key_lists, qd, kv, left, right, far[c][0], far[c][1], *extra_args)
        received.append((
            shifted(to_right, SEQ, 1), shifted(to_left, SEQ, -1),
            shifted(to_late, SEQ, FRAME_DEV), shifted(to_early, SEQ, -FRAME_DEV),
        ))
    from_left, from_right, from_early, from_late = (
        jnp.concatenate([r[k] for r in received], axis=-1) for k in range(4)
    )
    side = jnp.concatenate([from_left, from_right], axis=1).astype(F32)
    total = own + side + from_late.astype(F32) + from_early.astype(F32)
    grads = total.astype(BF16)
    return (d_queries, grads[0], grads[1])


def solution(mesh):
    groups, seq = mesh.devices.shape
    paired = Mesh(mesh.devices.reshape(groups, seq // 2, 2), ("groups",) + SEQ)
    spec = P(("groups",) + SEQ, None)
    return jax.shard_map(
        body,
        mesh=paired,
        in_specs=(spec, spec, spec, spec, spec),
        out_specs=(spec, spec, spec),
        check_vma=False,
    )
```

```python
import math

import jax
import jax.numpy as jnp
from jax import lax
from jax.experimental import pallas as pl
from jax.experimental.pallas import tpu as pltpu
from jax.sharding import PartitionSpec as P

BLK = 128
LOCAL_HEADS = 16
HEAD_SIZE = 128
FRAME_DEV = 4
BLK_DEV = 2
STEP_HEADS = 4
CHUNKS = ((4, 3), (2, 2))

NT = (((1,), (1,)), ((), ()))
TN = (((0,), (0,)), ((), ()))
F32 = jnp.float32
BF16 = jnp.bfloat16


def shifted(tree, axis, distance):
    count = lax.axis_size(axis)
    route = [(i, (i + distance) % count) for i in range(count)]
    return lax.ppermute(tree, axis, route)


def cols(hh):
    return slice(hh * HEAD_SIZE, (hh + 1) * HEAD_SIZE)


def picked(index):
    return pl.ds(pl.multiple_of(index * BLK, BLK), BLK)


def attend_kernel(kl_ref, qd_ref, kv_ref, left_ref, right_ref, early_ref, late_ref, *rest,
                  scale, aliased, step_heads):
    if aliased:
        rest = rest[2:]
    dq_ref, own_ref, to_left, to_right, to_early, to_late, acc_early, acc_late = rest
    acc_early[...] = jnp.zeros_like(acc_early)
    acc_late[...] = jnp.zeros_like(acc_late)
    for i in range(BLK_DEV):
        rows = slice(i * BLK, (i + 1) * BLK)
        side = left_ref if i == 0 else right_ref
        to_side = to_left if i == 0 else to_right
        early = lax.rem(kl_ref[i, 2], BLK_DEV)
        late = lax.rem(kl_ref[i, 3], BLK_DEV)
        for hh in range(step_heads):
            c = cols(hh)
            q = qd_ref[0, rows, c]
            do = qd_ref[1, rows, c]
            parts = []
            for n in range(2):
                parts.append(jnp.concatenate(
                    [kv_ref[n, rows, c], side[n, :, c], early_ref[n, picked(early), c],
                     late_ref[n, picked(late), c]], axis=0
                ))
            keys, vals = parts
            s = lax.dot_general(keys, q, NT, preferred_element_type=F32) * scale
            top = jnp.max(s, axis=0, keepdims=True)
            lse = top + jnp.log(jnp.sum(jnp.exp(s - top), axis=0, keepdims=True))
            p = jnp.exp(s - lse)
            p_low = p.astype(BF16)
            dp = lax.dot_general(vals, do, NT, preferred_element_type=F32)
            delta = jnp.sum(p_low.astype(F32) * dp, axis=0, keepdims=True)
            ds = (p * (dp - delta)).astype(BF16)
            dq = lax.dot_general(ds, keys, TN, preferred_element_type=F32) * scale
            dq_ref[rows, c] = dq.astype(BF16)
            d_key = jnp.dot(ds, q, preferred_element_type=F32) * scale
            d_value = jnp.dot(p_low, do, preferred_element_type=F32)
            for n, term in ((0, d_key), (1, d_value)):
                own_ref[n, rows, c] = term[0:BLK]
                to_side[n, :, c] = term[BLK:2 * BLK].astype(BF16)
                acc_early[n, picked(early), c] += term[2 * BLK:3 * BLK]
                acc_late[n, picked(late), c] += term[3 * BLK:4 * BLK]
    to_early[...] = acc_early[...].astype(BF16)
    to_late[...] = acc_late[...].astype(BF16)


def body(queries, keys, values, d_out, key_lists):
    rows, width = queries.shape
    steps = width // (HEAD_SIZE * STEP_HEADS)
    assert rows == BLK_DEV * BLK and key_lists.shape[0] == BLK_DEV
    assert steps * HEAD_SIZE * STEP_HEADS == width
    scale = 1.0 / math.sqrt(HEAD_SIZE)

    kv = jnp.stack([keys, values])
    qd = jnp.stack([queries, d_out])
    spans = [step_heads * HEAD_SIZE * count for step_heads, count in CHUNKS]
    starts = [sum(spans[:c]) for c in range(len(CHUNKS))]
    assert sum(spans) == width
    chunked = [kv[:, :, a:a + n] for a, n in zip(starts, spans)]
    far = []
    for part in chunked:
        far.append((shifted(part, "seq", FRAME_DEV), shifted(part, "seq", -FRAME_DEV)))
    left = shifted(kv[:, rows - BLK:], "seq", 1)
    right = shifted(kv[:, :BLK], "seq", -1)

    d_queries = own = None
    received = []
    for c, (step_heads, chunk_steps) in enumerate(CHUNKS):
        width_step = HEAD_SIZE * step_heads
        base = starts[c] // width_step
        chunk_width = spans[c]
        heads = chunk_steps * step_heads
        cost = pl.CostEstimate(
            flops=2 * BLK * 4 * BLK * HEAD_SIZE * 5 * BLK_DEV * heads,
            transcendentals=2 * BLK * 4 * BLK * BLK_DEV * heads,
            bytes_accessed=14 * rows * chunk_width * 2,
        )
        pair = pl.BlockSpec((2, rows, width_step), lambda h, *_, b=base: (0, 0, b + h))
        edge = pl.BlockSpec((2, BLK, width_step), lambda h, *_, b=base: (0, 0, b + h))
        out = pl.BlockSpec((rows, width_step), lambda h, *_, b=base: (0, b + h))
        local_pair = pl.BlockSpec((2, rows, width_step), lambda h, *_: (0, 0, h))
        local_edge = pl.BlockSpec((2, BLK, width_step), lambda h, *_: (0, 0, h))
        aliased = c > 0
        extra_specs = [pl.BlockSpec(memory_space=pl.ANY)] * 2 if aliased else []
        extra_args = [d_queries, own] if aliased else []
        aliases = {7: 0, 8: 1} if aliased else {}
        d_queries, own, to_left, to_right, to_early, to_late = pl.pallas_call(
            lambda *refs, a=aliased, k=step_heads: attend_kernel(
                *refs, scale=scale, aliased=a, step_heads=k),
            grid_spec=pltpu.PrefetchScalarGridSpec(
                num_scalar_prefetch=1,
                grid=(chunk_steps,),
                in_specs=[pair, pair, edge, edge, local_pair, local_pair] + extra_specs,
                out_specs=[out, pair, local_edge, local_edge, local_pair, local_pair],
                scratch_shapes=[pltpu.VMEM((2, rows, width_step), F32)] * 2,
            ),
            out_shape=[
                jax.ShapeDtypeStruct((rows, width), BF16),
                jax.ShapeDtypeStruct((2, rows, width), F32),
                jax.ShapeDtypeStruct((2, BLK, chunk_width), BF16),
                jax.ShapeDtypeStruct((2, BLK, chunk_width), BF16),
                jax.ShapeDtypeStruct((2, rows, chunk_width), BF16),
                jax.ShapeDtypeStruct((2, rows, chunk_width), BF16),
            ],
            input_output_aliases=aliases,
            cost_estimate=cost,
        )(key_lists, qd, kv, left, right, far[c][0], far[c][1], *extra_args)
        received.append((
            shifted(to_right, "seq", 1), shifted(to_left, "seq", -1),
            shifted(to_late, "seq", FRAME_DEV), shifted(to_early, "seq", -FRAME_DEV),
        ))
    from_left, from_right, from_early, from_late = (
        jnp.concatenate([r[k] for r in received], axis=-1) for k in range(4)
    )
    side = jnp.concatenate([from_left, from_right], axis=1).astype(F32)
    total = own + side + from_late.astype(F32) + from_early.astype(F32)
    grads = total.astype(BF16)
    return (d_queries, grads[0], grads[1])


def solution(mesh):
    spec = P(("groups", "seq"), None)
    return jax.shard_map(
        body,
        mesh=mesh,
        in_specs=(spec, spec, spec, spec, spec),
        out_specs=(spec, spec, spec),
        check_vma=False,
    )
```

```python
import math

import jax
import jax.numpy as jnp
from jax import lax
from jax.experimental import pallas as pl
from jax.experimental.pallas import tpu as pltpu
from jax.sharding import PartitionSpec as P

BLK = 128
LOCAL_HEADS = 16
HEAD_SIZE = 128
FRAME_DEV = 4
BLK_DEV = 2
STEP_HEADS = 4
CHUNKS = ((4, 3), (2, 2))

NT = (((1,), (1,)), ((), ()))
TN = (((0,), (0,)), ((), ()))
F32 = jnp.float32
BF16 = jnp.bfloat16


def shifted(tree, axis, distance):
    count = lax.axis_size(axis)
    route = [(i, (i + distance) % count) for i in range(count)]
    return lax.ppermute(tree, axis, route)


def cols(hh):
    return slice(hh * HEAD_SIZE, (hh + 1) * HEAD_SIZE)


def picked(index):
    return pl.ds(pl.multiple_of(index * BLK, BLK), BLK)


def attend_kernel(kl_ref, qd_ref, kv_ref, left_ref, right_ref, early_ref, late_ref, *rest,
                  scale, aliased, step_heads):
    if aliased:
        rest = rest[2:]
    dq_ref, own_ref, to_left, to_right, to_early, to_late, acc_early, acc_late = rest
    acc_early[...] = jnp.zeros_like(acc_early)
    acc_late[...] = jnp.zeros_like(acc_late)
    for i in range(BLK_DEV):
        rows = slice(i * BLK, (i + 1) * BLK)
        side = left_ref if i == 0 else right_ref
        to_side = to_left if i == 0 else to_right
        early = lax.rem(kl_ref[i, 2], BLK_DEV)
        late = lax.rem(kl_ref[i, 3], BLK_DEV)
        for hh in range(step_heads):
            c = cols(hh)
            q = qd_ref[0, rows, c]
            do = qd_ref[1, rows, c]
            parts = []
            for n in range(2):
                parts.append(jnp.concatenate(
                    [kv_ref[n, rows, c], side[n, :, c], early_ref[n, picked(early), c],
                     late_ref[n, picked(late), c]], axis=0
                ))
            keys, vals = parts
            s = lax.dot_general(keys, q, NT, preferred_element_type=F32) * scale
            top = jnp.max(s, axis=0, keepdims=True)
            lse = top + jnp.log(jnp.sum(jnp.exp(s - top), axis=0, keepdims=True))
            p = jnp.exp(s - lse)
            p_low = p.astype(BF16)
            dp = lax.dot_general(vals, do, NT, preferred_element_type=F32)
            delta = jnp.sum(p_low.astype(F32) * dp, axis=0, keepdims=True)
            ds = (p * (dp - delta)).astype(BF16)
            dq = lax.dot_general(ds, keys, TN, preferred_element_type=F32) * scale
            dq_ref[rows, c] = dq.astype(BF16)
            d_key = jnp.dot(ds, q, preferred_element_type=F32) * scale
            d_value = jnp.dot(p_low, do, preferred_element_type=F32)
            for n, term in ((0, d_key), (1, d_value)):
                own_ref[n, rows, c] = term[0:BLK]
                to_side[n, :, c] = term[BLK:2 * BLK].astype(BF16)
                acc_early[n, picked(early), c] += term[2 * BLK:3 * BLK]
                acc_late[n, picked(late), c] += term[3 * BLK:4 * BLK]
    to_early[...] = acc_early[...].astype(BF16)
    to_late[...] = acc_late[...].astype(BF16)


def body(queries, keys, values, d_out, key_lists):
    rows, width = queries.shape
    steps = width // (HEAD_SIZE * STEP_HEADS)
    assert rows == BLK_DEV * BLK and key_lists.shape[0] == BLK_DEV
    assert steps * HEAD_SIZE * STEP_HEADS == width
    scale = 1.0 / math.sqrt(HEAD_SIZE)

    kv = jnp.stack([keys, values])
    qd = jnp.stack([queries, d_out])
    spans = [step_heads * HEAD_SIZE * count for step_heads, count in CHUNKS]
    starts = [sum(spans[:c]) for c in range(len(CHUNKS))]
    assert sum(spans) == width
    chunked = [kv[:, :, a:a + n] for a, n in zip(starts, spans)]
    far = []
    for part in chunked:
        far.append((shifted(part, "seq", FRAME_DEV), shifted(part, "seq", -FRAME_DEV)))
    left = shifted(kv[:, rows - BLK:], "seq", 1)
    right = shifted(kv[:, :BLK], "seq", -1)

    d_queries = own = None
    received = []
    for c, (step_heads, chunk_steps) in enumerate(CHUNKS):
        width_step = HEAD_SIZE * step_heads
        base = starts[c] // width_step
        chunk_width = spans[c]
        heads = chunk_steps * step_heads
        cost = pl.CostEstimate(
            flops=2 * BLK * 4 * BLK * HEAD_SIZE * 5 * BLK_DEV * heads,
            transcendentals=2 * BLK * 4 * BLK * BLK_DEV * heads,
            bytes_accessed=14 * rows * chunk_width * 2,
        )
        pair = pl.BlockSpec((2, rows, width_step), lambda h, *_, b=base: (0, 0, b + h))
        edge = pl.BlockSpec((2, BLK, width_step), lambda h, *_, b=base: (0, 0, b + h))
        out = pl.BlockSpec((rows, width_step), lambda h, *_, b=base: (0, b + h))
        local_pair = pl.BlockSpec((2, rows, width_step), lambda h, *_: (0, 0, h))
        local_edge = pl.BlockSpec((2, BLK, width_step), lambda h, *_: (0, 0, h))
        aliased = c > 0
        extra_specs = [pl.BlockSpec(memory_space=pl.ANY)] * 2 if aliased else []
        extra_args = [d_queries, own] if aliased else []
        aliases = {7: 0, 8: 1} if aliased else {}
        d_queries, own, to_left, to_right, to_early, to_late = pl.pallas_call(
            lambda *refs, a=aliased, k=step_heads: attend_kernel(
                *refs, scale=scale, aliased=a, step_heads=k),
            grid_spec=pltpu.PrefetchScalarGridSpec(
                num_scalar_prefetch=1,
                grid=(chunk_steps,),
                in_specs=[pair, pair, edge, edge, local_pair, local_pair] + extra_specs,
                out_specs=[out, pair, local_edge, local_edge, local_pair, local_pair],
                scratch_shapes=[pltpu.VMEM((2, rows, width_step), F32)] * 2,
            ),
            out_shape=[
                jax.ShapeDtypeStruct((rows, width), BF16),
                jax.ShapeDtypeStruct((2, rows, width), F32),
                jax.ShapeDtypeStruct((2, BLK, chunk_width), BF16),
                jax.ShapeDtypeStruct((2, BLK, chunk_width), BF16),
                jax.ShapeDtypeStruct((2, rows, chunk_width), BF16),
                jax.ShapeDtypeStruct((2, rows, chunk_width), BF16),
            ],
            input_output_aliases=aliases,
            cost_estimate=cost,
        )(key_lists, qd, kv, left, right, far[c][0], far[c][1], *extra_args)
        received.append((
            shifted(to_right, "seq", 1), shifted(to_left, "seq", -1),
            shifted(to_late, "seq", FRAME_DEV), shifted(to_early, "seq", -FRAME_DEV),
        ))
    from_left, from_right, from_late = (
        jnp.concatenate([r[k] for r in received], axis=-1) for k in (0, 1, 3)
    )
    side = jnp.concatenate([from_left, from_right], axis=1).astype(F32)
    settled = [r[2] for r in received[:-1]]
    early_settled = jnp.concatenate(
        settled + [jnp.zeros_like(received[-1][2])], axis=-1
    ).astype(F32)
    partial = lax.optimization_barrier(own + side + from_late.astype(F32) + early_settled)
    last = jnp.concatenate(
        [jnp.zeros(r[2].shape, BF16) for r in received[:-1]] + [received[-1][2]], axis=-1
    )
    grads = [(partial[n] + last[n].astype(F32)).astype(BF16) for n in range(2)]
    return (d_queries, grads[0], grads[1])


def solution(mesh):
    spec = P(("groups", "seq"), None)
    return jax.shard_map(
        body,
        mesh=mesh,
        in_specs=(spec, spec, spec, spec, spec),
        out_specs=(spec, spec, spec),
        check_vma=False,
    )
```

```python
import math

import jax
import jax.numpy as jnp
from jax import lax
from jax.experimental import pallas as pl
from jax.experimental.pallas import tpu as pltpu
from jax.sharding import Mesh, PartitionSpec as P

BLK = 128
LOCAL_HEADS = 16
HEAD_SIZE = 128
FRAME_DEV = 4
BLK_DEV = 2
STEP_HEADS = 4
CHUNK_STEPS = (3, 1)

NT = (((1,), (1,)), ((), ()))
TN = (((0,), (0,)), ((), ()))
F32 = jnp.float32
BF16 = jnp.bfloat16


SEQ = ("pair", "core")


def crossing(tree):
    count = lax.axis_size(SEQ)
    route = [(i, (i - 1 if i % 2 == 0 else i + 1) % count) for i in range(count)]
    return lax.ppermute(tree, SEQ, route)


def swap_edges(for_left, for_right):
    core = lax.axis_index("core")
    even = core == 0
    across = crossing(jnp.where(even, for_left, for_right))
    gathered = lax.all_gather(jnp.where(even, for_right, for_left), "core")
    partner = lax.dynamic_index_in_dim(gathered, 1 - core, keepdims=False)
    return jnp.where(even, across, partner), jnp.where(even, partner, across)


def shifted(tree, axis, distance):
    count = lax.axis_size(axis)
    route = [(i, (i + distance) % count) for i in range(count)]
    return lax.ppermute(tree, axis, route)


def cols(hh):
    return slice(hh * HEAD_SIZE, (hh + 1) * HEAD_SIZE)


def picked(index):
    return pl.ds(pl.multiple_of(index * BLK, BLK), BLK)


def attend_kernel(kl_ref, qd_ref, kv_ref, left_ref, right_ref, early_ref, late_ref, *rest,
                  scale, aliased):
    if aliased:
        rest = rest[2:]
    dq_ref, own_ref, to_left, to_right, to_early, to_late, acc_early, acc_late = rest
    acc_early[...] = jnp.zeros_like(acc_early)
    acc_late[...] = jnp.zeros_like(acc_late)
    for i in range(BLK_DEV):
        rows = slice(i * BLK, (i + 1) * BLK)
        side = left_ref if i == 0 else right_ref
        to_side = to_left if i == 0 else to_right
        early = lax.rem(kl_ref[i, 2], BLK_DEV)
        late = lax.rem(kl_ref[i, 3], BLK_DEV)
        for hh in range(STEP_HEADS):
            c = cols(hh)
            q = qd_ref[0, rows, c]
            do = qd_ref[1, rows, c]
            parts = []
            for n in range(2):
                parts.append(jnp.concatenate(
                    [kv_ref[n, rows, c], side[n, :, c], early_ref[n, picked(early), c],
                     late_ref[n, picked(late), c]], axis=0
                ))
            keys, vals = parts
            s = lax.dot_general(keys, q, NT, preferred_element_type=F32) * scale
            top = jnp.max(s, axis=0, keepdims=True)
            lse = top + jnp.log(jnp.sum(jnp.exp(s - top), axis=0, keepdims=True))
            p = jnp.exp(s - lse)
            p_low = p.astype(BF16)
            dp = lax.dot_general(vals, do, NT, preferred_element_type=F32)
            delta = jnp.sum(p_low.astype(F32) * dp, axis=0, keepdims=True)
            ds = (p * (dp - delta)).astype(BF16)
            dq = lax.dot_general(ds, keys, TN, preferred_element_type=F32) * scale
            dq_ref[rows, c] = dq.astype(BF16)
            d_key = jnp.dot(ds, q, preferred_element_type=F32) * scale
            d_value = jnp.dot(p_low, do, preferred_element_type=F32)
            for n, term in ((0, d_key), (1, d_value)):
                own_ref[n, rows, c] = term[0:BLK]
                to_side[n, :, c] = term[BLK:2 * BLK].astype(BF16)
                acc_early[n, picked(early), c] += term[2 * BLK:3 * BLK]
                acc_late[n, picked(late), c] += term[3 * BLK:4 * BLK]
    to_early[...] = acc_early[...].astype(BF16)
    to_late[...] = acc_late[...].astype(BF16)


def body(queries, keys, values, d_out, key_lists):
    rows, width = queries.shape
    steps = width // (HEAD_SIZE * STEP_HEADS)
    assert rows == BLK_DEV * BLK and key_lists.shape[0] == BLK_DEV
    assert steps * HEAD_SIZE * STEP_HEADS == width
    scale = 1.0 / math.sqrt(HEAD_SIZE)

    kv = jnp.stack([keys, values])
    qd = jnp.stack([queries, d_out])
    width_step = HEAD_SIZE * STEP_HEADS
    assert sum(CHUNK_STEPS) == steps
    bases = [sum(CHUNK_STEPS[:c]) for c in range(len(CHUNK_STEPS))]
    chunked = [kv[:, :, b * width_step:(b + n) * width_step] for b, n in zip(bases, CHUNK_STEPS)]
    far = []
    for part in chunked:
        far.append((shifted(part, SEQ, FRAME_DEV), shifted(part, SEQ, -FRAME_DEV)))
    left, right = swap_edges(kv[:, :BLK], kv[:, rows - BLK:])

    d_queries = own = None
    received = []
    for c, (base, chunk_steps) in enumerate(zip(bases, CHUNK_STEPS)):
        chunk_width = chunk_steps * width_step
        heads = chunk_steps * STEP_HEADS
        cost = pl.CostEstimate(
            flops=2 * BLK * 4 * BLK * HEAD_SIZE * 5 * BLK_DEV * heads,
            transcendentals=2 * BLK * 4 * BLK * BLK_DEV * heads,
            bytes_accessed=14 * rows * chunk_width * 2,
        )
        pair = pl.BlockSpec((2, rows, width_step), lambda h, *_, b=base: (0, 0, b + h))
        edge = pl.BlockSpec((2, BLK, width_step), lambda h, *_, b=base: (0, 0, b + h))
        out = pl.BlockSpec((rows, width_step), lambda h, *_, b=base: (0, b + h))
        local_pair = pl.BlockSpec((2, rows, width_step), lambda h, *_: (0, 0, h))
        local_edge = pl.BlockSpec((2, BLK, width_step), lambda h, *_: (0, 0, h))
        aliased = c > 0
        extra_specs = [pl.BlockSpec(memory_space=pl.ANY)] * 2 if aliased else []
        extra_args = [d_queries, own] if aliased else []
        aliases = {7: 0, 8: 1} if aliased else {}
        d_queries, own, to_left, to_right, to_early, to_late = pl.pallas_call(
            lambda *refs, a=aliased: attend_kernel(*refs, scale=scale, aliased=a),
            grid_spec=pltpu.PrefetchScalarGridSpec(
                num_scalar_prefetch=1,
                grid=(chunk_steps,),
                in_specs=[pair, pair, edge, edge, local_pair, local_pair] + extra_specs,
                out_specs=[out, pair, local_edge, local_edge, local_pair, local_pair],
                scratch_shapes=[pltpu.VMEM((2, rows, width_step), F32)] * 2,
            ),
            out_shape=[
                jax.ShapeDtypeStruct((rows, width), BF16),
                jax.ShapeDtypeStruct((2, rows, width), F32),
                jax.ShapeDtypeStruct((2, BLK, chunk_width), BF16),
                jax.ShapeDtypeStruct((2, BLK, chunk_width), BF16),
                jax.ShapeDtypeStruct((2, rows, chunk_width), BF16),
                jax.ShapeDtypeStruct((2, rows, chunk_width), BF16),
            ],
            input_output_aliases=aliases,
            cost_estimate=cost,
        )(key_lists, qd, kv, left, right, far[c][0], far[c][1], *extra_args)
        received.append([
            (to_left, to_right),
            shifted(to_late, SEQ, FRAME_DEV), shifted(to_early, SEQ, -FRAME_DEV),
        ])
    tied = lax.optimization_barrier(([r[0] for r in received], d_queries, own))
    sides, d_queries, own = tied
    for r, (to_left, to_right) in zip(received, sides):
        from_left, from_right = swap_edges(to_left, to_right)
        r[0:1] = [from_left, from_right]
    from_left, from_right, from_early, from_late = (
        jnp.concatenate([r[k] for r in received], axis=-1) for k in range(4)
    )
    side = jnp.concatenate([from_left, from_right], axis=1).astype(F32)
    total = own + side + from_late.astype(F32) + from_early.astype(F32)
    grads = total.astype(BF16)
    return (d_queries, grads[0], grads[1])


def solution(mesh):
    groups, seq = mesh.devices.shape
    paired = Mesh(mesh.devices.reshape(groups, seq // 2, 2), ("groups",) + SEQ)
    spec = P(("groups",) + SEQ, None)
    return jax.shard_map(
        body,
        mesh=paired,
        in_specs=(spec, spec, spec, spec, spec),
        out_specs=(spec, spec, spec),
        check_vma=False,
    )
```

```python
import math

import jax
import jax.numpy as jnp
from jax import lax
from jax.experimental import pallas as pl
from jax.experimental.pallas import tpu as pltpu
from jax.sharding import PartitionSpec as P

BLK = 128
LOCAL_HEADS = 16
HEAD_SIZE = 128
FRAME_DEV = 4
BLK_DEV = 2
STEP_HEADS = 4
CHUNK_STEPS = (3, 1)

NT = (((1,), (1,)), ((), ()))
TN = (((0,), (0,)), ((), ()))
F32 = jnp.float32
BF16 = jnp.bfloat16


def paired_route(tree, step_even, step_odd):
    count = lax.axis_size("seq")
    route = [(i, (i + (step_even if i % 2 == 0 else step_odd)) % count) for i in range(count)]
    return lax.ppermute(tree, "seq", route)


def swap_edges(for_left, for_right):
    even = lax.rem(lax.axis_index("seq"), 2) == 0
    across = paired_route(jnp.where(even, for_left, for_right), -1, 1)
    beside = paired_route(jnp.where(even, for_right, for_left), 1, -1)
    return jnp.where(even, across, beside), jnp.where(even, beside, across)


def shifted(tree, axis, distance):
    count = lax.axis_size(axis)
    route = [(i, (i + distance) % count) for i in range(count)]
    return lax.ppermute(tree, axis, route)


def cols(hh):
    return slice(hh * HEAD_SIZE, (hh + 1) * HEAD_SIZE)


def picked(index):
    return pl.ds(pl.multiple_of(index * BLK, BLK), BLK)


def attend_kernel(kl_ref, qd_ref, kv_ref, left_ref, right_ref, early_ref, late_ref, *rest,
                  scale, aliased):
    if aliased:
        rest = rest[2:]
    dq_ref, own_ref, to_left, to_right, to_early, to_late, acc_early, acc_late = rest
    acc_early[...] = jnp.zeros_like(acc_early)
    acc_late[...] = jnp.zeros_like(acc_late)
    for i in range(BLK_DEV):
        rows = slice(i * BLK, (i + 1) * BLK)
        side = left_ref if i == 0 else right_ref
        to_side = to_left if i == 0 else to_right
        early = lax.rem(kl_ref[i, 2], BLK_DEV)
        late = lax.rem(kl_ref[i, 3], BLK_DEV)
        for hh in range(STEP_HEADS):
            c = cols(hh)
            q = qd_ref[0, rows, c]
            do = qd_ref[1, rows, c]
            parts = []
            for n in range(2):
                parts.append(jnp.concatenate(
                    [kv_ref[n, rows, c], side[n, :, c], early_ref[n, picked(early), c],
                     late_ref[n, picked(late), c]], axis=0
                ))
            keys, vals = parts
            s = lax.dot_general(keys, q, NT, preferred_element_type=F32) * scale
            top = jnp.max(s, axis=0, keepdims=True)
            lse = top + jnp.log(jnp.sum(jnp.exp(s - top), axis=0, keepdims=True))
            p = jnp.exp(s - lse)
            p_low = p.astype(BF16)
            dp = lax.dot_general(vals, do, NT, preferred_element_type=F32)
            delta = jnp.sum(p_low.astype(F32) * dp, axis=0, keepdims=True)
            ds = (p * (dp - delta)).astype(BF16)
            dq = lax.dot_general(ds, keys, TN, preferred_element_type=F32) * scale
            dq_ref[rows, c] = dq.astype(BF16)
            d_key = jnp.dot(ds, q, preferred_element_type=F32) * scale
            d_value = jnp.dot(p_low, do, preferred_element_type=F32)
            for n, term in ((0, d_key), (1, d_value)):
                own_ref[n, rows, c] = term[0:BLK]
                to_side[n, :, c] = term[BLK:2 * BLK].astype(BF16)
                acc_early[n, picked(early), c] += term[2 * BLK:3 * BLK]
                acc_late[n, picked(late), c] += term[3 * BLK:4 * BLK]
    to_early[...] = acc_early[...].astype(BF16)
    to_late[...] = acc_late[...].astype(BF16)


def body(queries, keys, values, d_out, key_lists):
    rows, width = queries.shape
    steps = width // (HEAD_SIZE * STEP_HEADS)
    assert rows == BLK_DEV * BLK and key_lists.shape[0] == BLK_DEV
    assert steps * HEAD_SIZE * STEP_HEADS == width
    scale = 1.0 / math.sqrt(HEAD_SIZE)

    kv = jnp.stack([keys, values])
    qd = jnp.stack([queries, d_out])
    width_step = HEAD_SIZE * STEP_HEADS
    assert sum(CHUNK_STEPS) == steps
    bases = [sum(CHUNK_STEPS[:c]) for c in range(len(CHUNK_STEPS))]
    chunked = [kv[:, :, b * width_step:(b + n) * width_step] for b, n in zip(bases, CHUNK_STEPS)]
    far = []
    for part in chunked:
        far.append((shifted(part, "seq", FRAME_DEV), shifted(part, "seq", -FRAME_DEV)))
    left, right = swap_edges(kv[:, :BLK], kv[:, rows - BLK:])

    d_queries = own = None
    received = []
    for c, (base, chunk_steps) in enumerate(zip(bases, CHUNK_STEPS)):
        chunk_width = chunk_steps * width_step
        heads = chunk_steps * STEP_HEADS
        cost = pl.CostEstimate(
            flops=2 * BLK * 4 * BLK * HEAD_SIZE * 5 * BLK_DEV * heads,
            transcendentals=2 * BLK * 4 * BLK * BLK_DEV * heads,
            bytes_accessed=14 * rows * chunk_width * 2,
        )
        pair = pl.BlockSpec((2, rows, width_step), lambda h, *_, b=base: (0, 0, b + h))
        edge = pl.BlockSpec((2, BLK, width_step), lambda h, *_, b=base: (0, 0, b + h))
        out = pl.BlockSpec((rows, width_step), lambda h, *_, b=base: (0, b + h))
        local_pair = pl.BlockSpec((2, rows, width_step), lambda h, *_: (0, 0, h))
        local_edge = pl.BlockSpec((2, BLK, width_step), lambda h, *_: (0, 0, h))
        aliased = c > 0
        extra_specs = [pl.BlockSpec(memory_space=pl.ANY)] * 2 if aliased else []
        extra_args = [d_queries, own] if aliased else []
        aliases = {7: 0, 8: 1} if aliased else {}
        d_queries, own, to_left, to_right, to_early, to_late = pl.pallas_call(
            lambda *refs, a=aliased: attend_kernel(*refs, scale=scale, aliased=a),
            grid_spec=pltpu.PrefetchScalarGridSpec(
                num_scalar_prefetch=1,
                grid=(chunk_steps,),
                in_specs=[pair, pair, edge, edge, local_pair, local_pair] + extra_specs,
                out_specs=[out, pair, local_edge, local_edge, local_pair, local_pair],
                scratch_shapes=[pltpu.VMEM((2, rows, width_step), F32)] * 2,
            ),
            out_shape=[
                jax.ShapeDtypeStruct((rows, width), BF16),
                jax.ShapeDtypeStruct((2, rows, width), F32),
                jax.ShapeDtypeStruct((2, BLK, chunk_width), BF16),
                jax.ShapeDtypeStruct((2, BLK, chunk_width), BF16),
                jax.ShapeDtypeStruct((2, rows, chunk_width), BF16),
                jax.ShapeDtypeStruct((2, rows, chunk_width), BF16),
            ],
            input_output_aliases=aliases,
            cost_estimate=cost,
        )(key_lists, qd, kv, left, right, far[c][0], far[c][1], *extra_args)
        received.append((
            *swap_edges(to_left, to_right),
            shifted(to_late, "seq", FRAME_DEV), shifted(to_early, "seq", -FRAME_DEV),
        ))
    from_left, from_right, from_early, from_late = (
        jnp.concatenate([r[k] for r in received], axis=-1) for k in range(4)
    )
    side = jnp.concatenate([from_left, from_right], axis=1).astype(F32)
    total = own + side + from_late.astype(F32) + from_early.astype(F32)
    grads = total.astype(BF16)
    return (d_queries, grads[0], grads[1])


def solution(mesh):
    spec = P(("groups", "seq"), None)
    return jax.shard_map(
        body,
        mesh=mesh,
        in_specs=(spec, spec, spec, spec, spec),
        out_specs=(spec, spec, spec),
        check_vma=False,
    )
```
